32 devices in a mesh: row: 8 (over z, y), col: 4 (over x, core).
Axes of the slice: x: 2, y: 2, z: 4, core: 2. Of those that a mesh axis runs over, the one named last changes fastest.
Arguments:
- design: bfloat16 [256, 24576], P('row', 'col'), may hold values from -0.375 to 0.375
- filter_taps: float32 [256], replicated, may hold values from -0.21875 to 0.21875
- probes: float32 [24576, 128], P('row', 'col'), may hold values from -576 to 576
- lower_bound: float32 [1], replicated, may hold values from 6 to 24
- upper_bound: float32 [1], replicated, may hold values from 192 to 288
Outputs:
- normal: float32 [24576, 24576], P('row', 'col')
- solution: float32 [24576, 128], P('row', 'col')
The draws below stay inside these ranges and needn't reach their ends.
All inputs are finite; a program needn't handle non-finite values.
Results may differ from the reference program's by a relative error of at most 0.0072.
The reference program's roundings to bfloat16 on the way (of `filter_matrix` and `white`) count: a program that leaves them out, or rounds other values in their place, can miss the bound.
Values may be sent and summed in bfloat16 or wider, within the bound.
No kernel may reach another device: no remote copies, remote signals or barrier semaphores. Data moves between devices by JAX's collectives and lax.ppermute only.
A program may use at most 128 MiB of HBM per device.

```python
import jax
import jax.numpy as jnp
from jax import lax

P_SIZE = 24576
EPOCHS = 256
NPROBE = 128
SWEEPS = 2


def level_of(rng, shape, pieces, low, high):
    factor_of, own = 1.0, jax.random.fold_in(rng, 6)
    for dim, blocks in pieces:
        steps = jnp.exp(jax.random.uniform(jax.random.fold_in(own, dim), (blocks,), jnp.float32, low / len(pieces), high / len(pieces)))
        factor_of = factor_of * jnp.repeat(steps, shape[dim] // blocks).reshape([-1 if axis == dim else 1 for axis in range(len(shape))])
    return factor_of


def gaussian(rng, extent, spread, reach, shards=(), held_as=jnp.bfloat16):
    array = spread * jax.random.normal(rng, extent, jnp.float32)
    if shards:
        array = array * level_of(rng, extent, shards, -0.22, 0.18)
    return jnp.clip(array, -reach, reach).astype(held_as)


def setup_inputs(seed: int = 0) -> dict:
    key_of = jax.random.split(jax.random.key(seed), 6)
    design = gaussian(key_of[0], (EPOCHS, P_SIZE), EPOCHS ** -0.5, 0.375, ((0, 8), (1, 4)))
    filter_taps = gaussian(key_of[1], (EPOCHS,), (3 * EPOCHS) ** -0.5, 0.21875, (), jnp.float32)
    probes = gaussian(key_of[2], (P_SIZE, NPROBE), (P_SIZE // EPOCHS), 576.0, ((0, 8), (1, 4)), jnp.float32)
    lower_bound = jnp.clip(jax.random.uniform(key_of[3], (1,), jnp.float32, 6.0, 24.0), 6.0, 24.0)
    upper_bound = jnp.clip(jax.random.uniform(key_of[4], (1,), jnp.float32, 192.0, 288.0), 192.0, 288.0)
    return {"design": design, "filter_taps": filter_taps, "probes": probes, "lower_bound": lower_bound, "upper_bound": upper_bound}


def whitening(filter_taps):
    count = filter_taps.shape[0]
    padded = jnp.concatenate([filter_taps, jnp.zeros_like(filter_taps)])
    repeated = jnp.tile(padded, count)[:count * (2 * count - 1)]
    upper = repeated.reshape(count, 2 * count - 1)[:, :count]
    matrix = upper.T + jnp.eye(count, dtype=filter_taps.dtype)
    return matrix.astype(jnp.bfloat16)


def reference(design, filter_taps, probes, lower_bound, upper_bound):
    filter_matrix = whitening(filter_taps)
    white = jnp.dot(filter_matrix, design, preferred_element_type=jnp.float32).astype(jnp.bfloat16)
    normal = lax.dot_general(white, white, (((0,), (0,)), ((), ())), preferred_element_type=jnp.float32)
    jacobi = (jnp.sum(jnp.square(white.astype(jnp.float32)), axis=0) + 1e-6)[:, None]
    center_value = (lower_bound[0] + upper_bound[0]) / 2.0
    half_width = (upper_bound[0] - lower_bound[0]) / 2.0
    sigma_value = center_value / half_width
    weight_now = 1.0 / sigma_value
    residual = probes
    direction = residual / jacobi / center_value
    solution = jnp.zeros_like(probes)
    for sweep_index in range(SWEEPS):
        solution = solution + direction
        residual = residual - jnp.dot(normal, direction, precision=lax.Precision.HIGHEST)
        weight_next = 1.0 / (2.0 * sigma_value - weight_now)
        direction = weight_next * weight_now * direction + (2.0 * weight_next / half_width) * (residual / jacobi)
        weight_now = weight_next
    solution = solution + direction
    return normal, solution
```

```python
import jax
import jax.numpy as jnp
from jax import lax
from jax.sharding import PartitionSpec as P

SWEEPS = 2


def whitening(filter_taps):
    count = filter_taps.shape[0]
    padded = jnp.concatenate([filter_taps, jnp.zeros_like(filter_taps)])
    repeated = jnp.tile(padded, count)[: count * (2 * count - 1)]
    upper = repeated.reshape(count, 2 * count - 1)[:, :count]
    matrix = upper.T + jnp.eye(count, dtype=filter_taps.dtype)
    return matrix.astype(jnp.bfloat16)


def is_power_of_two(count):
    return count > 0 and count & (count - 1) == 0


def swap(block, axis, count, bit):
    return lax.ppermute(block, axis, [(i, i ^ bit) for i in range(count)])


def tree_sum(block, axis):
    count = lax.axis_size(axis)
    if not is_power_of_two(count):
        return lax.psum(block, axis)
    bit = 1
    while bit < count:
        block = block + swap(block, axis, count, bit)
        bit *= 2
    return block


def tree_broadcast(block, axis, owner):
    count = lax.axis_size(axis)
    offset = lax.axis_index(axis) ^ owner
    if not is_power_of_two(count):
        block = jnp.where(offset == 0, block, jnp.zeros_like(block))
        return lax.psum(block, axis)
    bit = 1
    while bit < count:
        arrived = swap(block, axis, count, bit)
        block = jnp.where(offset // bit == 1, arrived, block)
        bit *= 2
    return block


def contract_epochs(left, right):
    return lax.dot_general(
        left, right, (((0,), (0,)), ((), ())), precision=lax.Precision.HIGHEST
    )


def body(design, filter_taps, probes, lower_bound, upper_bound):
    row_count = lax.axis_size("row")
    col_count = lax.axis_size("col")
    fold_ratio = row_count // col_count
    row_index = lax.axis_index("row")
    panel_width = design.shape[1]
    row_width = panel_width // fold_ratio
    filter_matrix = whitening(filter_taps)
    whole_panel = lax.all_gather(design, "row", axis=0, tiled=True)
    white = jnp.dot(filter_matrix, whole_panel, preferred_element_type=jnp.float32).astype(
        jnp.bfloat16
    )
    own_slice = lax.dynamic_slice_in_dim(white, row_index % fold_ratio * row_width, row_width, 1)
    panel = tree_broadcast(own_slice, "col", row_index // fold_ratio)
    normal_tile = lax.dot_general(
        panel, white, (((0,), (0,)), ((), ())), preferred_element_type=jnp.float32
    )
    white_wide = white.astype(jnp.float32)
    panel_jacobi = jnp.sum(jnp.square(white_wide), axis=0) + 1e-06
    coupling = jnp.dot(
        white_wide / panel_jacobi[None, :], white_wide.T, precision=lax.Precision.HIGHEST
    )
    coupling = tree_sum(coupling, "col")
    panel_wide = panel.astype(jnp.float32)
    jacobi = (jnp.sum(jnp.square(panel_wide), axis=0) + 1e-06)[:, None]
    center_value = (lower_bound[0] + upper_bound[0]) / 2.0
    half_width = (upper_bound[0] - lower_bound[0]) / 2.0
    sigma_value = center_value / half_width
    weight_now = 1.0 / sigma_value
    residual = probes
    scaled = residual / jacobi
    direction = scaled / center_value
    scaled_image = tree_sum(jnp.dot(panel_wide, scaled, precision=lax.Precision.HIGHEST), "row")
    image = scaled_image / center_value
    solution = jnp.zeros_like(residual)
    for sweep_index in range(SWEEPS):
        solution = solution + direction
        residual = residual - contract_epochs(panel_wide, image)
        weight_next = 1.0 / (2.0 * sigma_value - weight_now)
        direction = weight_next * weight_now * direction + 2.0 * weight_next / half_width * (
            residual / jacobi
        )
        if sweep_index + 1 < SWEEPS:
            scaled_image = scaled_image - jnp.dot(
                coupling, image, precision=lax.Precision.HIGHEST
            )
            image = weight_next * weight_now * image + 2.0 * weight_next / half_width * scaled_image
        weight_now = weight_next
    solution = solution + direction
    return (normal_tile, solution)


def solution(mesh):
    placed = (P("row", "col"), P(), P("row", "col"), P(), P())
    return jax.shard_map(
        body,
        mesh=mesh,
        in_specs=placed,
        out_specs=(P("row", "col"), P("row", "col")),
        check_vma=False,
    )
```

```python
import jax
import jax.numpy as jnp
from jax import lax
from jax.sharding import PartitionSpec as P

SWEEPS = 2


def whitening(filter_taps):
    count = filter_taps.shape[0]
    padded = jnp.concatenate([filter_taps, jnp.zeros_like(filter_taps)])
    repeated = jnp.tile(padded, count)[: count * (2 * count - 1)]
    upper = repeated.reshape(count, 2 * count - 1)[:, :count]
    matrix = upper.T + jnp.eye(count, dtype=filter_taps.dtype)
    return matrix.astype(jnp.bfloat16)


def is_power_of_two(count):
    return count > 0 and count & (count - 1) == 0


def swap(block, axis, count, bit):
    return lax.ppermute(block, axis, [(i, i ^ bit) for i in range(count)])


def tree_sum(block, axis):
    count = lax.axis_size(axis)
    if not is_power_of_two(count):
        return lax.psum(block, axis)
    bit = 1
    while bit < count:
        block = block + swap(block, axis, count, bit)
        bit *= 2
    return block


def tree_broadcast(block, fold_ratio):
    row_count = lax.axis_size("row")
    col_count = lax.axis_size("col")
    owner = lax.axis_index("row") // fold_ratio
    offset = lax.axis_index("col") ^ owner
    if not is_power_of_two(col_count):
        block = jnp.where(offset == 0, block, jnp.zeros_like(block))
        return lax.psum(block, "col")
    bits = [1 << k for k in range(1, col_count.bit_length() - 1)] + [1][: col_count > 1]
    done = 0
    for bit in bits:
        pairs = []
        for row in range(row_count):
            base = row * col_count
            row_owner = row // fold_ratio
            for held in range(col_count):
                if (held ^ row_owner) & ~done == 0:
                    pairs.append((base + held, base + (held ^ bit)))
        arrived = lax.ppermute(block, ("row", "col"), pairs)
        done |= bit
        block = jnp.where((offset & ~done == 0) & (offset & bit != 0), arrived, block)
    return block


def contract_epochs(left, right):
    return lax.dot_general(
        left, right, (((0,), (0,)), ((), ())), precision=lax.Precision.HIGHEST
    )


def body(design, filter_taps, probes, lower_bound, upper_bound):
    row_count = lax.axis_size("row")
    col_count = lax.axis_size("col")
    fold_ratio = row_count // col_count
    row_index = lax.axis_index("row")
    panel_width = design.shape[1]
    row_width = panel_width // fold_ratio
    filter_matrix = whitening(filter_taps)

    epoch_block = design.shape[0]
    epochs = epoch_block * row_count
    part_width = row_width // 2
    slices = design.reshape(epoch_block, fold_ratio, row_width)
    owned = row_index % fold_ratio
    gathered = []
    for part_index in range(2):
        part = slices[:, :, part_index * part_width : (part_index + 1) * part_width]
        part = part.reshape(epoch_block, fold_ratio * part_width)
        gathered.append(lax.all_gather(part, "row", axis=0, tiled=True))
    parts, panel_parts = [], []
    for part_index in range(2):
        whole = gathered[part_index]
        if panel_parts:
            whole, panel_parts[-1] = lax.optimization_barrier((whole, panel_parts[-1]))
        part = jnp.dot(filter_matrix, whole, preferred_element_type=jnp.float32)
        part = part.astype(jnp.bfloat16).reshape(epochs, fold_ratio, part_width)
        parts.append(part)
        own_slice = lax.dynamic_index_in_dim(part, owned, 1, keepdims=False)
        panel_parts.append(tree_broadcast(own_slice, fold_ratio))
    white = jnp.stack(parts, axis=2).reshape(epochs, panel_width)
    panel = jnp.concatenate(panel_parts, axis=1)
    normal_tile = lax.dot_general(
        panel, white, (((0,), (0,)), ((), ())), preferred_element_type=jnp.float32
    )
    white_wide = white.astype(jnp.float32)
    panel_jacobi = jnp.sum(jnp.square(white_wide), axis=0) + 1e-06
    coupling = jnp.dot(
        white_wide / panel_jacobi[None, :], white_wide.T, precision=lax.Precision.HIGHEST
    )
    coupling = tree_sum(coupling, "col")
    panel_wide = panel.astype(jnp.float32)
    jacobi = (jnp.sum(jnp.square(panel_wide), axis=0) + 1e-06)[:, None]
    center_value = (lower_bound[0] + upper_bound[0]) / 2.0
    half_width = (upper_bound[0] - lower_bound[0]) / 2.0
    sigma_value = center_value / half_width
    weight_now = 1.0 / sigma_value
    residual = probes
    scaled = residual / jacobi
    direction = scaled / center_value
    scaled_image = tree_sum(jnp.dot(panel_wide, scaled, precision=lax.Precision.HIGHEST), "row")
    image = scaled_image / center_value
    solution = jnp.zeros_like(residual)
    for sweep_index in range(SWEEPS):
        solution = solution + direction
        residual = residual - contract_epochs(panel_wide, image)
        weight_next = 1.0 / (2.0 * sigma_value - weight_now)
        direction = weight_next * weight_now * direction + 2.0 * weight_next / half_width * (
            residual / jacobi
        )
        if sweep_index + 1 < SWEEPS:
            scaled_image = scaled_image - jnp.dot(
                coupling, image, precision=lax.Precision.HIGHEST
            )
            image = weight_next * weight_now * image + 2.0 * weight_next / half_width * scaled_image
        weight_now = weight_next
    solution = solution + direction
    return (normal_tile, solution)


def solution(mesh):
    placed = (P("row", "col"), P(), P("row", "col"), P(), P())
    return jax.shard_map(
        body,
        mesh=mesh,
        in_specs=placed,
        out_specs=(P("row", "col"), P("row", "col")),
        check_vma=False,
    )
```

```python
import jax
import jax.numpy as jnp
from jax import lax
from jax.sharding import PartitionSpec as P

SWEEPS = 2


def whitening(filter_taps):
    count = filter_taps.shape[0]
    padded = jnp.concatenate([filter_taps, jnp.zeros_like(filter_taps)])
    repeated = jnp.tile(padded, count)[: count * (2 * count - 1)]
    upper = repeated.reshape(count, 2 * count - 1)[:, :count]
    matrix = upper.T + jnp.eye(count, dtype=filter_taps.dtype)
    return matrix.astype(jnp.bfloat16)


def is_power_of_two(count):
    return count > 0 and count & (count - 1) == 0


def swap(block, axis, count, bit):
    return lax.ppermute(block, axis, [(i, i ^ bit) for i in range(count)])


def tree_sum(block, axis):
    count = lax.axis_size(axis)
    if not is_power_of_two(count):
        return lax.psum(block, axis)
    bit = 1
    while bit < count:
        block = block + swap(block, axis, count, bit)
        bit *= 2
    return block


def shift_sum(block, axis):
    count = lax.axis_size(axis)
    arrived = [
        lax.ppermute(block, axis, [(i, (i + shift) % count) for i in range(count)])
        for shift in range(1, count)
    ]
    for other in arrived:
        block = block + other
    return block


def tree_broadcast(block, fold_ratio):
    row_count = lax.axis_size("row")
    col_count = lax.axis_size("col")
    owner = lax.axis_index("row") // fold_ratio
    offset = lax.axis_index("col") ^ owner
    if not is_power_of_two(col_count):
        block = jnp.where(offset == 0, block, jnp.zeros_like(block))
        return lax.psum(block, "col")
    bits = [1 << k for k in range(1, col_count.bit_length() - 1)] + [1][: col_count > 1]
    done = 0
    for bit in bits:
        pairs = []
        for row in range(row_count):
            base = row * col_count
            row_owner = row // fold_ratio
            for held in range(col_count):
                if (held ^ row_owner) & ~done == 0:
                    pairs.append((base + held, base + (held ^ bit)))
        arrived = lax.ppermute(block, ("row", "col"), pairs)
        done |= bit
        block = jnp.where((offset & ~done == 0) & (offset & bit != 0), arrived, block)
    return block


def contract_epochs(left, right):
    return lax.dot_general(
        left, right, (((0,), (0,)), ((), ())), precision=lax.Precision.HIGHEST
    )


def body(design, filter_taps, probes, lower_bound, upper_bound):
    row_count = lax.axis_size("row")
    col_count = lax.axis_size("col")
    fold_ratio = row_count // col_count
    row_index = lax.axis_index("row")
    panel_width = design.shape[1]
    row_width = panel_width // fold_ratio
    filter_matrix = whitening(filter_taps)
    whole_panel = lax.all_gather(design, "row", axis=0, tiled=True)
    white = jnp.dot(filter_matrix, whole_panel, preferred_element_type=jnp.float32).astype(
        jnp.bfloat16
    )
    own_slice = lax.dynamic_slice_in_dim(white, row_index % fold_ratio * row_width, row_width, 1)
    panel = tree_broadcast(own_slice, fold_ratio)
    normal_tile = lax.dot_general(
        panel, white, (((0,), (0,)), ((), ())), preferred_element_type=jnp.float32
    )
    white_wide = white.astype(jnp.float32)
    panel_jacobi = jnp.sum(jnp.square(white_wide), axis=0) + 1e-06
    coupling = jnp.dot(
        white_wide / panel_jacobi[None, :], white_wide.T, precision=lax.Precision.HIGHEST
    )
    coupling = tree_sum(coupling, "col")
    panel_wide = panel.astype(jnp.float32)
    jacobi = (jnp.sum(jnp.square(panel_wide), axis=0) + 1e-06)[:, None]
    center_value = (lower_bound[0] + upper_bound[0]) / 2.0
    half_width = (upper_bound[0] - lower_bound[0]) / 2.0
    sigma_value = center_value / half_width
    weight_now = 1.0 / sigma_value
    residual = probes
    scaled = residual / jacobi
    direction = scaled / center_value
    scaled_image = shift_sum(jnp.dot(panel_wide, scaled, precision=lax.Precision.HIGHEST), "row")
    image = scaled_image / center_value
    solution = jnp.zeros_like(residual)
    for sweep_index in range(SWEEPS):
        solution = solution + direction
        residual = residual - contract_epochs(panel_wide, image)
        weight_next = 1.0 / (2.0 * sigma_value - weight_now)
        direction = weight_next * weight_now * direction + 2.0 * weight_next / half_width * (
            residual / jacobi
        )
        if sweep_index + 1 < SWEEPS:
            scaled_image = scaled_image - jnp.dot(
                coupling, image, precision=lax.Precision.HIGHEST
            )
            image = weight_next * weight_now * image + 2.0 * weight_next / half_width * scaled_image
        weight_now = weight_next
    solution = solution + direction
    return (normal_tile, solution)


def solution(mesh):
    placed = (P("row", "col"), P(), P("row", "col"), P(), P())
    return jax.shard_map(
        body,
        mesh=mesh,
        in_specs=placed,
        out_specs=(P("row", "col"), P("row", "col")),
        check_vma=False,
    )
```

```python
import jax
import jax.numpy as jnp
from jax import lax
from jax.sharding import PartitionSpec as P

SWEEPS = 2


def whitening(filter_taps):
    count = filter_taps.shape[0]
    padded = jnp.concatenate([filter_taps, jnp.zeros_like(filter_taps)])
    repeated = jnp.tile(padded, count)[: count * (2 * count - 1)]
    upper = repeated.reshape(count, 2 * count - 1)[:, :count]
    matrix = upper.T + jnp.eye(count, dtype=filter_taps.dtype)
    return matrix.astype(jnp.bfloat16)


def is_power_of_two(count):
    return count > 0 and count & (count - 1) == 0


def swap(block, axis, count, bit):
    return lax.ppermute(block, axis, [(i, i ^ bit) for i in range(count)])


def tree_sum(block, axis):
    count = lax.axis_size(axis)
    if not is_power_of_two(count):
        return lax.psum(block, axis)
    bit = 1
    while bit < count:
        block = block + swap(block, axis, count, bit)
        bit *= 2
    return block


def shift_sum(block, axis):
    count = lax.axis_size(axis)
    arrived = [
        lax.ppermute(block, axis, [(i, (i + shift) % count) for i in range(count)])
        for shift in range(1, count)
    ]
    for other in arrived:
        block = block + other
    return block


def tree_broadcast(block, fold_ratio, companion):
    row_count = lax.axis_size("row")
    col_count = lax.axis_size("col")
    owner = lax.axis_index("row") // fold_ratio
    offset = lax.axis_index("col") ^ owner
    if not is_power_of_two(col_count):
        block = jnp.where(offset == 0, block, jnp.zeros_like(block))
        return lax.psum(block, "col"), companion()
    bits = [1 << k for k in range(1, col_count.bit_length() - 1)] + [1][: col_count > 1]
    done = 0
    for bit in bits:
        pairs = []
        for row in range(row_count):
            base = row * col_count
            row_owner = row // fold_ratio
            for held in range(col_count):
                if (held ^ row_owner) & ~done == 0:
                    pairs.append((base + held, base + (held ^ bit)))
        arrived = lax.ppermute(block, ("row", "col"), pairs)
        done |= bit
        block = jnp.where((offset & ~done == 0) & (offset & bit != 0), arrived, block)
        block, companion = lax.optimization_barrier((block, companion()))
        companion = lambda held=companion: held
    return block, companion()


def contract_epochs(left, right):
    return lax.dot_general(
        left, right, (((0,), (0,)), ((), ())), precision=lax.Precision.HIGHEST
    )


def body(design, filter_taps, probes, lower_bound, upper_bound):
    row_count = lax.axis_size("row")
    col_count = lax.axis_size("col")
    fold_ratio = row_count // col_count
    row_index = lax.axis_index("row")
    panel_width = design.shape[1]
    row_width = panel_width // fold_ratio
    filter_matrix = whitening(filter_taps)
    whole_panel = lax.all_gather(design, "row", axis=0, tiled=True)
    white = jnp.dot(filter_matrix, whole_panel, preferred_element_type=jnp.float32).astype(
        jnp.bfloat16
    )
    own_slice = lax.dynamic_slice_in_dim(white, row_index % fold_ratio * row_width, row_width, 1)

    def couple():
        white_wide = white.astype(jnp.float32)
        panel_jacobi = jnp.sum(jnp.square(white_wide), axis=0) + 1e-06
        coupling = jnp.dot(
            white_wide / panel_jacobi[None, :], white_wide.T, precision=lax.Precision.HIGHEST
        )
        return tree_sum(coupling, "col")

    panel, coupling = tree_broadcast(own_slice, fold_ratio, couple)
    panel_wide = panel.astype(jnp.float32)
    normal_tile = lax.dot_general(
        panel, white, (((0,), (0,)), ((), ())), preferred_element_type=jnp.float32
    )
    jacobi = (jnp.sum(jnp.square(panel_wide), axis=0) + 1e-06)[:, None]
    center_value = (lower_bound[0] + upper_bound[0]) / 2.0
    half_width = (upper_bound[0] - lower_bound[0]) / 2.0
    sigma_value = center_value / half_width
    weight_now = 1.0 / sigma_value
    residual = probes
    scaled = residual / jacobi
    direction = scaled / center_value
    scaled_image = shift_sum(jnp.dot(panel_wide, scaled, precision=lax.Precision.HIGHEST), "row")
    image = scaled_image / center_value
    solution = jnp.zeros_like(residual)
    for sweep_index in range(SWEEPS):
        solution = solution + direction
        residual = residual - contract_epochs(panel_wide, image)
        weight_next = 1.0 / (2.0 * sigma_value - weight_now)
        direction = weight_next * weight_now * direction + 2.0 * weight_next / half_width * (
            residual / jacobi
        )
        if sweep_index + 1 < SWEEPS:
            scaled_image = scaled_image - jnp.dot(
                coupling, image, precision=lax.Precision.HIGHEST
            )
            image = weight_next * weight_now * image + 2.0 * weight_next / half_width * scaled_image
        weight_now = weight_next
    solution = solution + direction
    return (normal_tile, solution)


def solution(mesh):
    placed = (P("row", "col"), P(), P("row", "col"), P(), P())
    return jax.shard_map(
        body,
        mesh=mesh,
        in_specs=placed,
        out_specs=(P("row", "col"), P("row", "col")),
        check_vma=False,
    )
```

```python
import jax
import jax.numpy as jnp
from jax import lax
from jax.experimental import pallas as pl
from jax.experimental.pallas import tpu as pltpu
from jax.sharding import PartitionSpec as P

SWEEPS = 2


def whitening(filter_taps):
    count = filter_taps.shape[0]
    padded = jnp.concatenate([filter_taps, jnp.zeros_like(filter_taps)])
    repeated = jnp.tile(padded, count)[: count * (2 * count - 1)]
    upper = repeated.reshape(count, 2 * count - 1)[:, :count]
    matrix = upper.T + jnp.eye(count, dtype=filter_taps.dtype)
    return matrix.astype(jnp.bfloat16)


def is_power_of_two(count):
    return count > 0 and count & (count - 1) == 0


def swap(block, axis, count, bit):
    return lax.ppermute(block, axis, [(i, i ^ bit) for i in range(count)])


def tree_sum(block, axis):
    count = lax.axis_size(axis)
    if not is_power_of_two(count):
        return lax.psum(block, axis)
    bit = 1
    while bit < count:
        block = block + swap(block, axis, count, bit)
        bit *= 2
    return block


def shift_sum(block, axis):
    count = lax.axis_size(axis)
    arrived = [
        lax.ppermute(block, axis, [(i, (i + shift) % count) for i in range(count)])
        for shift in range(1, count)
    ]
    for other in arrived:
        block = block + other
    return block


def tree_broadcast(block, fold_ratio, companion, on_first=None):
    row_count = lax.axis_size("row")
    col_count = lax.axis_size("col")
    owner = lax.axis_index("row") // fold_ratio
    offset = lax.axis_index("col") ^ owner
    if not is_power_of_two(col_count):
        block = jnp.where(offset == 0, block, jnp.zeros_like(block))
        return lax.psum(block, "col"), companion()
    bits = [1 << k for k in range(1, col_count.bit_length() - 1)] + [1][: col_count > 1]
    done = 0
    for bit in bits:
        pairs = []
        for row in range(row_count):
            base = row * col_count
            row_owner = row // fold_ratio
            for held in range(col_count):
                if (held ^ row_owner) & ~done == 0:
                    pairs.append((base + held, base + (held ^ bit)))
        arrived = lax.ppermute(block, ("row", "col"), pairs)
        done |= bit
        block = jnp.where((offset & ~done == 0) & (offset & bit != 0), arrived, block)
        block, companion = lax.optimization_barrier((block, companion()))
        companion = lambda held=companion: held
        if on_first is not None:
            block = on_first(block)
            on_first = None
    return block, companion()


def product_kernel(left_ref, right_ref, out_ref):
    out_ref[...] = jnp.dot(left_ref[...], right_ref[...], preferred_element_type=jnp.float32)


def normal_rows(left, right, total_rows, first_row, previous):
    rows, epochs = left.shape
    width = right.shape[1]
    tile_rows = 512 if rows % 512 == 0 else rows
    tile_cols = 2048 if width % 2048 == 0 else width
    row_offset = first_row // tile_rows
    in_specs = [
        pl.BlockSpec((tile_rows, epochs), lambda j, i: (i, 0)),
        pl.BlockSpec((epochs, tile_cols), lambda j, i: (0, j)),
    ]
    operands = [left, right]
    aliases = {}
    if previous is not None:
        in_specs.append(pl.BlockSpec(memory_space=pl.ANY))
        operands.append(previous)
        aliases = {2: 0}

    def kernel(left_ref, right_ref, *rest):
        product_kernel(left_ref, right_ref, rest[-1])

    return pl.pallas_call(
        kernel,
        grid=(width // tile_cols, rows // tile_rows),
        in_specs=in_specs,
        out_specs=pl.BlockSpec((tile_rows, tile_cols), lambda j, i: (i + row_offset, j)),
        out_shape=jax.ShapeDtypeStruct((total_rows, width), jnp.float32),
        input_output_aliases=aliases,
        compiler_params=pltpu.CompilerParams(vmem_limit_bytes=48 * 1024 * 1024),
        cost_estimate=pl.CostEstimate(
            flops=2 * rows * epochs * width,
            transcendentals=0,
            bytes_accessed=rows * width * 4 + epochs * width * 2 + rows * epochs * 2,
        ),
    )(*operands)


def contract_epochs(left, right):
    return lax.dot_general(
        left, right, (((0,), (0,)), ((), ())), precision=lax.Precision.HIGHEST
    )


def body(design, filter_taps, probes, lower_bound, upper_bound):
    row_count = lax.axis_size("row")
    col_count = lax.axis_size("col")
    fold_ratio = row_count // col_count
    row_index = lax.axis_index("row")
    panel_width = design.shape[1]
    row_width = panel_width // fold_ratio
    filter_matrix = whitening(filter_taps)
    whole_panel = lax.all_gather(design, "row", axis=0, tiled=True)
    white = jnp.dot(filter_matrix, whole_panel, preferred_element_type=jnp.float32).astype(
        jnp.bfloat16
    )
    own_slice = lax.dynamic_slice_in_dim(white, row_index % fold_ratio * row_width, row_width, 1)

    def couple():
        white_wide = white.astype(jnp.float32)
        panel_jacobi = jnp.sum(jnp.square(white_wide), axis=0) + 1e-06
        coupling = jnp.dot(
            white_wide / panel_jacobi[None, :], white_wide.T, precision=lax.Precision.HIGHEST
        )
        return tree_sum(coupling, "col")

    half_rows = row_width // 2
    held = {}

    def release_second(block):
        held["second"], block = lax.optimization_barrier((own_slice[:, half_rows:], block))
        return block

    panel_first, coupling = tree_broadcast(
        own_slice[:, :half_rows], fold_ratio, couple, release_second
    )
    panel_second, normal_tile = tree_broadcast(
        held["second"],
        fold_ratio,
        lambda: normal_rows(panel_first.T, white, row_width, 0, None),
    )
    normal_tile = normal_rows(panel_second.T, white, row_width, half_rows, normal_tile)
    panel = jnp.concatenate([panel_first, panel_second], axis=1)
    panel_wide = panel.astype(jnp.float32)
    jacobi = (jnp.sum(jnp.square(panel_wide), axis=0) + 1e-06)[:, None]
    center_value = (lower_bound[0] + upper_bound[0]) / 2.0
    half_width = (upper_bound[0] - lower_bound[0]) / 2.0
    sigma_value = center_value / half_width
    weight_now = 1.0 / sigma_value
    residual = probes
    scaled = residual / jacobi
    direction = scaled / center_value
    scaled_image = shift_sum(jnp.dot(panel_wide, scaled, precision=lax.Precision.HIGHEST), "row")
    image = scaled_image / center_value
    solution = jnp.zeros_like(residual)
    for sweep_index in range(SWEEPS):
        solution = solution + direction
        residual = residual - contract_epochs(panel_wide, image)
        weight_next = 1.0 / (2.0 * sigma_value - weight_now)
        direction = weight_next * weight_now * direction + 2.0 * weight_next / half_width * (
            residual / jacobi
        )
        if sweep_index + 1 < SWEEPS:
            scaled_image = scaled_image - jnp.dot(
                coupling, image, precision=lax.Precision.HIGHEST
            )
            image = weight_next * weight_now * image + 2.0 * weight_next / half_width * scaled_image
        weight_now = weight_next
    solution = solution + direction
    return (normal_tile, solution)


def solution(mesh):
    placed = (P("row", "col"), P(), P("row", "col"), P(), P())
    return jax.shard_map(
        body,
        mesh=mesh,
        in_specs=placed,
        out_specs=(P("row", "col"), P("row", "col")),
        check_vma=False,
    )
```

```python
import jax
import jax.numpy as jnp
from jax import lax
from jax.experimental import pallas as pl
from jax.experimental.pallas import tpu as pltpu
from jax.sharding import PartitionSpec as P

SWEEPS = 2


def whitening(filter_taps):
    count = filter_taps.shape[0]
    padded = jnp.concatenate([filter_taps, jnp.zeros_like(filter_taps)])
    repeated = jnp.tile(padded, count)[: count * (2 * count - 1)]
    upper = repeated.reshape(count, 2 * count - 1)[:, :count]
    matrix = upper.T + jnp.eye(count, dtype=filter_taps.dtype)
    return matrix.astype(jnp.bfloat16)


def is_power_of_two(count):
    return count > 0 and count & (count - 1) == 0


def swap(block, axis, count, bit):
    return lax.ppermute(block, axis, [(i, i ^ bit) for i in range(count)])


def tree_sum(block, axis):
    count = lax.axis_size(axis)
    if not is_power_of_two(count):
        return lax.psum(block, axis)
    bit = 1
    while bit < count:
        block = block + swap(block, axis, count, bit)
        bit *= 2
    return block


def shift_sum(block, axis):
    count = lax.axis_size(axis)
    arrived = [
        lax.ppermute(block, axis, [(i, (i + shift) % count) for i in range(count)])
        for shift in range(1, count)
    ]
    for other in arrived:
        block = block + other
    return block


def tree_broadcast(block, fold_ratio, companion, on_first=None):
    row_count = lax.axis_size("row")
    col_count = lax.axis_size("col")
    owner = lax.axis_index("row") // fold_ratio
    offset = lax.axis_index("col") ^ owner
    if not is_power_of_two(col_count):
        block = jnp.where(offset == 0, block, jnp.zeros_like(block))
        return lax.psum(block, "col"), companion()
    bits = [1 << k for k in range(1, col_count.bit_length() - 1)] + [1][: col_count > 1]
    done = 0
    for bit in bits:
        pairs = []
        for row in range(row_count):
            base = row * col_count
            row_owner = row // fold_ratio
            for held in range(col_count):
                if (held ^ row_owner) & ~done == 0:
                    pairs.append((base + held, base + (held ^ bit)))
        arrived = lax.ppermute(block, ("row", "col"), pairs)
        done |= bit
        block = jnp.where((offset & ~done == 0) & (offset & bit != 0), arrived, block)
        block, companion = lax.optimization_barrier((block, companion()))
        companion = lambda held=companion: held
        if on_first is not None:
            block = on_first(block)
            on_first = None
    return block, companion()


def product_kernel(left_ref, right_ref, out_ref):
    out_ref[...] = lax.dot_general(
        left_ref[...], right_ref[...], (((0,), (0,)), ((), ())), preferred_element_type=jnp.float32
    )


def normal_rows(left, right, total_rows, first_row, previous):
    epochs, rows = left.shape
    width = right.shape[1]
    tile_rows = 512 if rows % 512 == 0 else rows
    tile_cols = 2048 if width % 2048 == 0 else width
    row_offset = first_row // tile_rows
    in_specs = [
        pl.BlockSpec((epochs, tile_rows), lambda j, i: (0, i)),
        pl.BlockSpec((epochs, tile_cols), lambda j, i: (0, j)),
    ]
    operands = [left, right]
    aliases = {}
    if previous is not None:
        in_specs.append(pl.BlockSpec(memory_space=pl.ANY))
        operands.append(previous)
        aliases = {2: 0}

    def kernel(left_ref, right_ref, *rest):
        product_kernel(left_ref, right_ref, rest[-1])

    return pl.pallas_call(
        kernel,
        grid=(width // tile_cols, rows // tile_rows),
        in_specs=in_specs,
        out_specs=pl.BlockSpec((tile_rows, tile_cols), lambda j, i: (i + row_offset, j)),
        out_shape=jax.ShapeDtypeStruct((total_rows, width), jnp.float32),
        input_output_aliases=aliases,
        compiler_params=pltpu.CompilerParams(vmem_limit_bytes=48 * 1024 * 1024),
        cost_estimate=pl.CostEstimate(
            flops=2 * rows * epochs * width,
            transcendentals=0,
            bytes_accessed=rows * width * 4 + epochs * width * 2 + rows * epochs * 2,
        ),
    )(*operands)


def contract_epochs(left, right):
    return lax.dot_general(
        left, right, (((0,), (0,)), ((), ())), precision=lax.Precision.HIGH
    )


def body(design, filter_taps, probes, lower_bound, upper_bound):
    row_count = lax.axis_size("row")
    col_count = lax.axis_size("col")
    fold_ratio = row_count // col_count
    row_index = lax.axis_index("row")
    panel_width = design.shape[1]
    row_width = panel_width // fold_ratio
    filter_matrix = whitening(filter_taps)
    whole_panel = lax.all_gather(design, "row", axis=0, tiled=True)
    white = jnp.dot(filter_matrix, whole_panel, preferred_element_type=jnp.float32).astype(
        jnp.bfloat16
    )
    own_slice = lax.dynamic_slice_in_dim(white, row_index % fold_ratio * row_width, row_width, 1)

    def couple():
        white_wide = white.astype(jnp.float32)
        panel_jacobi = jnp.sum(jnp.square(white_wide), axis=0) + 1e-06
        coupling = jnp.dot(
            white_wide / panel_jacobi[None, :], white_wide.T, precision=lax.Precision.HIGH
        )
        return tree_sum(coupling, "col")

    half_rows = row_width // 2
    held = {}

    def release_second(block):
        held["second"], block = lax.optimization_barrier((own_slice[:, half_rows:], block))
        return block

    panel_first, coupling = tree_broadcast(
        own_slice[:, :half_rows], fold_ratio, couple, release_second
    )
    panel_second, normal_tile = tree_broadcast(
        held["second"],
        fold_ratio,
        lambda: normal_rows(panel_first, white, row_width, 0, None),
    )
    normal_tile = normal_rows(panel_second, white, row_width, half_rows, normal_tile)
    panel = jnp.concatenate([panel_first, panel_second], axis=1)
    panel_wide = panel.astype(jnp.float32)
    jacobi = (jnp.sum(jnp.square(panel_wide), axis=0) + 1e-06)[:, None]
    center_value = (lower_bound[0] + upper_bound[0]) / 2.0
    half_width = (upper_bound[0] - lower_bound[0]) / 2.0
    sigma_value = center_value / half_width
    weight_now = 1.0 / sigma_value
    residual = probes
    scaled = residual / jacobi
    direction = scaled / center_value
    scaled_image = shift_sum(jnp.dot(panel_wide, scaled, precision=lax.Precision.HIGH), "row")
    image = scaled_image / center_value
    solution = jnp.zeros_like(residual)
    for sweep_index in range(SWEEPS):
        solution = solution + direction
        residual = residual - contract_epochs(panel_wide, image)
        weight_next = 1.0 / (2.0 * sigma_value - weight_now)
        direction = weight_next * weight_now * direction + 2.0 * weight_next / half_width * (
            residual / jacobi
        )
        if sweep_index + 1 < SWEEPS:
            scaled_image = scaled_image - jnp.dot(
                coupling, image, precision=lax.Precision.HIGH
            )
            image = weight_next * weight_now * image + 2.0 * weight_next / half_width * scaled_image
        weight_now = weight_next
    solution = solution + direction
    return (normal_tile, solution)


def solution(mesh):
    placed = (P("row", "col"), P(), P("row", "col"), P(), P())
    return jax.shard_map(
        body,
        mesh=mesh,
        in_specs=placed,
        out_specs=(P("row", "col"), P("row", "col")),
        check_vma=False,
    )
```

```python
import jax
import jax.numpy as jnp
from jax import lax
from jax.experimental import pallas as pl
from jax.experimental.pallas import tpu as pltpu
from jax.sharding import PartitionSpec as P

SWEEPS = 2


def whitening(filter_taps):
    count = filter_taps.shape[0]
    padded = jnp.concatenate([filter_taps, jnp.zeros_like(filter_taps)])
    repeated = jnp.tile(padded, count)[: count * (2 * count - 1)]
    upper = repeated.reshape(count, 2 * count - 1)[:, :count]
    matrix = upper.T + jnp.eye(count, dtype=filter_taps.dtype)
    return matrix.astype(jnp.bfloat16)


def is_power_of_two(count):
    return count > 0 and count & (count - 1) == 0


def swap(block, axis, count, bit):
    return lax.ppermute(block, axis, [(i, i ^ bit) for i in range(count)])


def tree_sum(block, axis):
    count = lax.axis_size(axis)
    if not is_power_of_two(count):
        return lax.psum(block, axis)
    bit = 1
    while bit < count:
        block = block + swap(block, axis, count, bit)
        bit *= 2
    return block


def shift_sum(block, axis):
    count = lax.axis_size(axis)
    arrived = [
        lax.ppermute(block, axis, [(i, (i + shift) % count) for i in range(count)])
        for shift in range(1, count)
    ]
    for other in arrived:
        block = block + other
    return block


def tree_broadcast(block, fold_ratio, companion, on_first=None):
    row_count = lax.axis_size("row")
    col_count = lax.axis_size("col")
    owner = lax.axis_index("row") // fold_ratio
    offset = lax.axis_index("col") ^ owner
    if not is_power_of_two(col_count):
        block = jnp.where(offset == 0, block, jnp.zeros_like(block))
        return lax.psum(block, "col"), companion()
    bits = [1 << k for k in range(1, col_count.bit_length() - 1)] + [1][: col_count > 1]
    done = 0
    for bit in bits:
        pairs = []
        for row in range(row_count):
            base = row * col_count
            row_owner = row // fold_ratio
            for held in range(col_count):
                if (held ^ row_owner) & ~done == 0:
                    pairs.append((base + held, base + (held ^ bit)))
        arrived = lax.ppermute(block, ("row", "col"), pairs)
        done |= bit
        block = jnp.where((offset & ~done == 0) & (offset & bit != 0), arrived, block)
        block, companion = lax.optimization_barrier((block, companion()))
        companion = lambda held=companion: held
        if on_first is not None:
            block = on_first(block)
            on_first = None
    return block, companion()


def product_kernel(left_ref, right_ref, out_ref):
    out_ref[...] = lax.dot_general(
        left_ref[...], right_ref[...], (((0,), (0,)), ((), ())), preferred_element_type=jnp.float32
    )


def normal_rows(left, right, total_rows, first_row, previous):
    epochs, rows = left.shape
    width = right.shape[1]
    tile_rows = 512 if rows % 512 == 0 else rows
    tile_cols = 2048 if width % 2048 == 0 else width
    row_offset = first_row // tile_rows
    in_specs = [
        pl.BlockSpec((epochs, tile_rows), lambda j, i: (0, i)),
        pl.BlockSpec((epochs, tile_cols), lambda j, i: (0, j)),
    ]
    operands = [left, right]
    aliases = {}
    if previous is not None:
        in_specs.append(pl.BlockSpec(memory_space=pl.ANY))
        operands.append(previous)
        aliases = {2: 0}

    def kernel(left_ref, right_ref, *rest):
        product_kernel(left_ref, right_ref, rest[-1])

    return pl.pallas_call(
        kernel,
        grid=(width // tile_cols, rows // tile_rows),
        in_specs=in_specs,
        out_specs=pl.BlockSpec((tile_rows, tile_cols), lambda j, i: (i + row_offset, j)),
        out_shape=jax.ShapeDtypeStruct((total_rows, width), jnp.float32),
        input_output_aliases=aliases,
        compiler_params=pltpu.CompilerParams(vmem_limit_bytes=48 * 1024 * 1024),
        cost_estimate=pl.CostEstimate(
            flops=2 * rows * epochs * width,
            transcendentals=0,
            bytes_accessed=rows * width * 4 + epochs * width * 2 + rows * epochs * 2,
        ),
    )(*operands)


def contract_epochs(left, right):
    return lax.dot_general(
        left, right, (((0,), (0,)), ((), ())), precision=lax.Precision.HIGH
    )


def body(design, filter_taps, probes, lower_bound, upper_bound):
    row_count = lax.axis_size("row")
    col_count = lax.axis_size("col")
    fold_ratio = row_count // col_count
    row_index = lax.axis_index("row")
    panel_width = design.shape[1]
    row_width = panel_width // fold_ratio
    filter_matrix = whitening(filter_taps)
    whole_panel = lax.all_gather(design, "row", axis=0, tiled=True)
    white = jnp.dot(filter_matrix, whole_panel, preferred_element_type=jnp.float32).astype(
        jnp.bfloat16
    )
    own_slice = lax.dynamic_slice_in_dim(white, row_index % fold_ratio * row_width, row_width, 1)

    def couple():
        white_wide = white.astype(jnp.float32)
        panel_jacobi = jnp.sum(jnp.square(white_wide), axis=0) + 1e-06
        coupling = jnp.dot(
            white_wide / panel_jacobi[None, :], white_wide.T, precision=lax.Precision.HIGH
        )
        return tree_sum(coupling, "col")

    half_rows = row_width // 2
    held = {}

    def release_second(block):
        held["second"], block = lax.optimization_barrier((own_slice[:, half_rows:], block))
        return block

    panel_first, coupling = tree_broadcast(
        own_slice[:, :half_rows], fold_ratio, couple, release_second
    )
    panel_second, normal_tile = tree_broadcast(
        held["second"],
        fold_ratio,
        lambda: normal_rows(panel_first, white, row_width, 0, None),
    )
    normal_tile = normal_rows(panel_second, white, row_width, half_rows, normal_tile)
    panel = jnp.concatenate([panel_first, panel_second], axis=1)
    panel_wide = panel.astype(jnp.float32)
    jacobi = (jnp.sum(jnp.square(panel_wide), axis=0) + 1e-06)[:, None]
    center_value = (lower_bound[0] + upper_bound[0]) / 2.0
    half_width = (upper_bound[0] - lower_bound[0]) / 2.0
    sigma_value = center_value / half_width
    weight_now = 1.0 / sigma_value
    residual = probes
    scaled = residual / jacobi
    direction = scaled / center_value
    scaled_image = tree_sum(jnp.dot(panel_wide, scaled, precision=lax.Precision.HIGH), "row")
    image = scaled_image / center_value
    solution = jnp.zeros_like(residual)
    for sweep_index in range(SWEEPS):
        solution = solution + direction
        residual = residual - contract_epochs(panel_wide, image)
        weight_next = 1.0 / (2.0 * sigma_value - weight_now)
        direction = weight_next * weight_now * direction + 2.0 * weight_next / half_width * (
            residual / jacobi
        )
        if sweep_index + 1 < SWEEPS:
            scaled_image = scaled_image - jnp.dot(
                coupling, image, precision=lax.Precision.HIGH
            )
            image = weight_next * weight_now * image + 2.0 * weight_next / half_width * scaled_image
        weight_now = weight_next
    solution = solution + direction
    return (normal_tile, solution)


def solution(mesh):
    placed = (P("row", "col"), P(), P("row", "col"), P(), P())
    return jax.shard_map(
        body,
        mesh=mesh,
        in_specs=placed,
        out_specs=(P("row", "col"), P("row", "col")),
        check_vma=False,
    )
```

```python
import jax
import jax.numpy as jnp
from jax import lax
from jax.experimental import pallas as pl
from jax.experimental.pallas import tpu as pltpu
from jax.sharding import PartitionSpec as P

SWEEPS = 2


def whitening(filter_taps):
    count = filter_taps.shape[0]
    padded = jnp.concatenate([filter_taps, jnp.zeros_like(filter_taps)])
    repeated = jnp.tile(padded, count)[: count * (2 * count - 1)]
    upper = repeated.reshape(count, 2 * count - 1)[:, :count]
    matrix = upper.T + jnp.eye(count, dtype=filter_taps.dtype)
    return matrix.astype(jnp.bfloat16)


def is_power_of_two(count):
    return count > 0 and count & (count - 1) == 0


def swap(block, axis, count, bit):
    return lax.ppermute(block, axis, [(i, i ^ bit) for i in range(count)])


def tree_sum(block, axis):
    count = lax.axis_size(axis)
    if not is_power_of_two(count):
        return lax.psum(block, axis)
    bit = 1
    while bit < count:
        block = block + swap(block, axis, count, bit)
        bit *= 2
    return block


def shift_sum(block, axis):
    count = lax.axis_size(axis)
    arrived = [
        lax.ppermute(block, axis, [(i, (i + shift) % count) for i in range(count)])
        for shift in range(1, count)
    ]
    for other in arrived:
        block = block + other
    return block


def tree_broadcast(block, fold_ratio, companion, on_first=None):
    row_count = lax.axis_size("row")
    col_count = lax.axis_size("col")
    owner = lax.axis_index("row") // fold_ratio
    offset = lax.axis_index("col") ^ owner
    if not is_power_of_two(col_count):
        block = jnp.where(offset == 0, block, jnp.zeros_like(block))
        return lax.psum(block, "col"), companion()
    bits = [1 << k for k in range(1, col_count.bit_length() - 1)] + [1][: col_count > 1]
    done = 0
    for bit in bits:
        pairs = []
        for row in range(row_count):
            base = row * col_count
            row_owner = row // fold_ratio
            for held in range(col_count):
                if (held ^ row_owner) & ~done == 0:
                    pairs.append((base + held, base + (held ^ bit)))
        arrived = lax.ppermute(block, ("row", "col"), pairs)
        done |= bit
        block = jnp.where((offset & ~done == 0) & (offset & bit != 0), arrived, block)
        block, companion = lax.optimization_barrier((block, companion()))
        companion = lambda held=companion: held
        if on_first is not None:
            block = on_first(block)
            on_first = None
    return block, companion()


def product_kernel(left_ref, right_ref, out_ref):
    out_ref[...] = lax.dot_general(
        left_ref[...], right_ref[...], (((0,), (0,)), ((), ())), preferred_element_type=jnp.float32
    )


def normal_rows(left, right, total_rows, first_row, previous):
    epochs, rows = left.shape
    width = right.shape[1]
    tile_rows = 512 if rows % 512 == 0 else rows
    tile_cols = 2048 if width % 2048 == 0 else width
    row_offset = first_row // tile_rows
    in_specs = [
        pl.BlockSpec((epochs, tile_rows), lambda j, i: (0, i)),
        pl.BlockSpec((epochs, tile_cols), lambda j, i: (0, j)),
    ]
    operands = [left, right]
    aliases = {}
    if previous is not None:
        in_specs.append(pl.BlockSpec(memory_space=pl.ANY))
        operands.append(previous)
        aliases = {2: 0}

    def kernel(left_ref, right_ref, *rest):
        product_kernel(left_ref, right_ref, rest[-1])

    return pl.pallas_call(
        kernel,
        grid=(width // tile_cols, rows // tile_rows),
        in_specs=in_specs,
        out_specs=pl.BlockSpec((tile_rows, tile_cols), lambda j, i: (i + row_offset, j)),
        out_shape=jax.ShapeDtypeStruct((total_rows, width), jnp.float32),
        input_output_aliases=aliases,
        compiler_params=pltpu.CompilerParams(vmem_limit_bytes=48 * 1024 * 1024),
        cost_estimate=pl.CostEstimate(
            flops=2 * rows * epochs * width,
            transcendentals=0,
            bytes_accessed=rows * width * 4 + epochs * width * 2 + rows * epochs * 2,
        ),
    )(*operands)


def contract_epochs(left, right):
    return lax.dot_general(
        left, right, (((0,), (0,)), ((), ())), precision=lax.Precision.HIGH
    )


def body(design, filter_taps, probes, lower_bound, upper_bound):
    row_count = lax.axis_size("row")
    col_count = lax.axis_size("col")
    fold_ratio = row_count // col_count
    row_index = lax.axis_index("row")
    panel_width = design.shape[1]
    row_width = panel_width // fold_ratio
    filter_matrix = whitening(filter_taps)
    whole_panel = lax.all_gather(design, "row", axis=0, tiled=True)
    white = jnp.dot(filter_matrix, whole_panel, preferred_element_type=jnp.float32).astype(
        jnp.bfloat16
    )
    own_slice = lax.dynamic_slice_in_dim(white, row_index % fold_ratio * row_width, row_width, 1)

    def couple():
        white_wide = white.astype(jnp.float32)
        panel_jacobi = jnp.sum(jnp.square(white_wide), axis=0) + 1e-06
        coupling = jnp.dot(
            white_wide / panel_jacobi[None, :], white_wide.T, precision=lax.Precision.HIGH
        )
        return tree_sum(coupling, "col")

    half_rows = row_width // 2
    held = {}

    def release_second(block):
        held["second"], block = lax.optimization_barrier((own_slice[:, half_rows:], block))
        return block

    panel_first, _ = tree_broadcast(
        own_slice[:, :half_rows], fold_ratio, lambda: (), release_second
    )
    panel_second, (normal_tile, coupling) = tree_broadcast(
        held["second"],
        fold_ratio,
        lambda: (normal_rows(panel_first, white, row_width, 0, None), couple()),
    )
    normal_tile = normal_rows(panel_second, white, row_width, half_rows, normal_tile)
    panel = jnp.concatenate([panel_first, panel_second], axis=1)
    panel_wide = panel.astype(jnp.float32)
    jacobi = (jnp.sum(jnp.square(panel_wide), axis=0) + 1e-06)[:, None]
    center_value = (lower_bound[0] + upper_bound[0]) / 2.0
    half_width = (upper_bound[0] - lower_bound[0]) / 2.0
    sigma_value = center_value / half_width
    weight_now = 1.0 / sigma_value
    residual = probes
    scaled = residual / jacobi
    direction = scaled / center_value
    scaled_image = tree_sum(jnp.dot(panel_wide, scaled, precision=lax.Precision.HIGH), "row")
    image = scaled_image / center_value
    solution = jnp.zeros_like(residual)
    for sweep_index in range(SWEEPS):
        solution = solution + direction
        residual = residual - contract_epochs(panel_wide, image)
        weight_next = 1.0 / (2.0 * sigma_value - weight_now)
        direction = weight_next * weight_now * direction + 2.0 * weight_next / half_width * (
            residual / jacobi
        )
        if sweep_index + 1 < SWEEPS:
            scaled_image = scaled_image - jnp.dot(
                coupling, image, precision=lax.Precision.HIGH
            )
            image = weight_next * weight_now * image + 2.0 * weight_next / half_width * scaled_image
        weight_now = weight_next
    solution = solution + direction
    return (normal_tile, solution)


def solution(mesh):
    placed = (P("row", "col"), P(), P("row", "col"), P(), P())
    return jax.shard_map(
        body,
        mesh=mesh,
        in_specs=placed,
        out_specs=(P("row", "col"), P("row", "col")),
        check_vma=False,
    )
```

```python
import jax
import jax.numpy as jnp
from jax import lax
from jax.experimental import pallas as pl
from jax.experimental.pallas import tpu as pltpu
from jax.sharding import PartitionSpec as P

SWEEPS = 2


def whitening(filter_taps):
    count = filter_taps.shape[0]
    padded = jnp.concatenate([filter_taps, jnp.zeros_like(filter_taps)])
    repeated = jnp.tile(padded, count)[: count * (2 * count - 1)]
    upper = repeated.reshape(count, 2 * count - 1)[:, :count]
    matrix = upper.T + jnp.eye(count, dtype=filter_taps.dtype)
    return matrix.astype(jnp.bfloat16)


def is_power_of_two(count):
    return count > 0 and count & (count - 1) == 0


def swap(block, axis, count, bit):
    return lax.ppermute(block, axis, [(i, i ^ bit) for i in range(count)])


def tree_sum(block, axis):
    count = lax.axis_size(axis)
    if not is_power_of_two(count):
        return lax.psum(block, axis)
    bit = 1
    while bit < count:
        block = block + swap(block, axis, count, bit)
        bit *= 2
    return block


def shift_sum(block, axis):
    count = lax.axis_size(axis)
    arrived = [
        lax.ppermute(block, axis, [(i, (i + shift) % count) for i in range(count)])
        for shift in range(1, count)
    ]
    for other in arrived:
        block = block + other
    return block


def tree_broadcast(block, fold_ratio, companion, on_first=None):
    row_count = lax.axis_size("row")
    col_count = lax.axis_size("col")
    owner = lax.axis_index("row") // fold_ratio
    offset = lax.axis_index("col") ^ owner
    if not is_power_of_two(col_count):
        block = jnp.where(offset == 0, block, jnp.zeros_like(block))
        return lax.psum(block, "col"), companion()
    bits = [1 << k for k in range(1, col_count.bit_length() - 1)] + [1][: col_count > 1]
    done = 0
    for bit in bits:
        pairs = []
        for row in range(row_count):
            base = row * col_count
            row_owner = row // fold_ratio
            for held in range(col_count):
                if (held ^ row_owner) & ~done == 0:
                    pairs.append((base + held, base + (held ^ bit)))
        arrived = lax.ppermute(block, ("row", "col"), pairs)
        done |= bit
        block = jnp.where((offset & ~done == 0) & (offset & bit != 0), arrived, block)
        block, companion = lax.optimization_barrier((block, companion()))
        companion = lambda held=companion: held
        if on_first is not None:
            block = on_first(block)
            on_first = None
    return block, companion()


def product_kernel(left_ref, right_ref, out_ref):
    out_ref[...] = lax.dot_general(
        left_ref[...], right_ref[...], (((0,), (0,)), ((), ())), preferred_element_type=jnp.float32
    )


def normal_rows(left, right, total_rows, first_row, previous):
    epochs, rows = left.shape
    width = right.shape[1]
    tile_rows = 512 if rows % 512 == 0 else rows
    tile_cols = 2048 if width % 2048 == 0 else width
    row_offset = first_row // tile_rows
    in_specs = [
        pl.BlockSpec((epochs, tile_rows), lambda j, i: (0, i)),
        pl.BlockSpec((epochs, tile_cols), lambda j, i: (0, j)),
    ]
    operands = [left, right]
    aliases = {}
    if previous is not None:
        in_specs.append(pl.BlockSpec(memory_space=pl.ANY))
        operands.append(previous)
        aliases = {2: 0}

    def kernel(left_ref, right_ref, *rest):
        product_kernel(left_ref, right_ref, rest[-1])

    return pl.pallas_call(
        kernel,
        grid=(width // tile_cols, rows // tile_rows),
        in_specs=in_specs,
        out_specs=pl.BlockSpec((tile_rows, tile_cols), lambda j, i: (i + row_offset, j)),
        out_shape=jax.ShapeDtypeStruct((total_rows, width), jnp.float32),
        input_output_aliases=aliases,
        compiler_params=pltpu.CompilerParams(vmem_limit_bytes=48 * 1024 * 1024),
        cost_estimate=pl.CostEstimate(
            flops=2 * rows * epochs * width,
            transcendentals=0,
            bytes_accessed=rows * width * 4 + epochs * width * 2 + rows * epochs * 2,
        ),
    )(*operands)


def contract_epochs(left, right):
    return lax.dot_general(
        left, right, (((0,), (0,)), ((), ())), precision=lax.Precision.HIGH
    )


def body(design, filter_taps, probes, lower_bound, upper_bound):
    row_count = lax.axis_size("row")
    col_count = lax.axis_size("col")
    fold_ratio = row_count // col_count
    row_index = lax.axis_index("row")
    panel_width = design.shape[1]
    row_width = panel_width // fold_ratio
    filter_matrix = whitening(filter_taps)
    whole_panel = lax.all_gather(design, "row", axis=0, tiled=True)
    white = jnp.dot(filter_matrix, whole_panel, preferred_element_type=jnp.float32).astype(
        jnp.bfloat16
    )
    own_slice = lax.dynamic_slice_in_dim(white, row_index % fold_ratio * row_width, row_width, 1)

    def couple():
        white_wide = held["white"].astype(jnp.float32)
        panel_jacobi = jnp.sum(jnp.square(white_wide), axis=0) + 1e-06
        coupling = jnp.dot(
            white_wide / panel_jacobi[None, :], white_wide.T, precision=lax.Precision.HIGH
        )
        return tree_sum(coupling, "col")

    half_rows = row_width // 2
    held = {}

    def release_second(block):
        held["second"], held["white"], block = lax.optimization_barrier(
            (own_slice[:, half_rows:], white, block)
        )
        return block

    panel_first, _ = tree_broadcast(
        own_slice[:, :half_rows], fold_ratio, lambda: (), release_second
    )
    coupling = couple()
    panel_second, normal_tile = tree_broadcast(
        held["second"],
        fold_ratio,
        lambda: normal_rows(panel_first, white, row_width, 0, None),
    )
    normal_tile = normal_rows(panel_second, white, row_width, half_rows, normal_tile)
    panel = jnp.concatenate([panel_first, panel_second], axis=1)
    panel_wide = panel.astype(jnp.float32)
    jacobi = (jnp.sum(jnp.square(panel_wide), axis=0) + 1e-06)[:, None]
    center_value = (lower_bound[0] + upper_bound[0]) / 2.0
    half_width = (upper_bound[0] - lower_bound[0]) / 2.0
    sigma_value = center_value / half_width
    weight_now = 1.0 / sigma_value
    residual = probes
    scaled = residual / jacobi
    direction = scaled / center_value
    scaled_image = tree_sum(jnp.dot(panel_wide, scaled, precision=lax.Precision.HIGH), "row")
    image = scaled_image / center_value
    solution = jnp.zeros_like(residual)
    for sweep_index in range(SWEEPS):
        solution = solution + direction
        residual = residual - contract_epochs(panel_wide, image)
        weight_next = 1.0 / (2.0 * sigma_value - weight_now)
        direction = weight_next * weight_now * direction + 2.0 * weight_next / half_width * (
            residual / jacobi
        )
        if sweep_index + 1 < SWEEPS:
            scaled_image = scaled_image - jnp.dot(
                coupling, image, precision=lax.Precision.HIGH
            )
            image = weight_next * weight_now * image + 2.0 * weight_next / half_width * scaled_image
        weight_now = weight_next
    solution = solution + direction
    return (normal_tile, solution)


def solution(mesh):
    placed = (P("row", "col"), P(), P("row", "col"), P(), P())
    return jax.shard_map(
        body,
        mesh=mesh,
        in_specs=placed,
        out_specs=(P("row", "col"), P("row", "col")),
        check_vma=False,
    )
```

```python
import jax
import jax.numpy as jnp
from jax import lax
from jax.experimental import pallas as pl
from jax.experimental.pallas import tpu as pltpu
from jax.sharding import PartitionSpec as P

SWEEPS = 2


def whitening(filter_taps):
    count = filter_taps.shape[0]
    padded = jnp.concatenate([filter_taps, jnp.zeros_like(filter_taps)])
    repeated = jnp.tile(padded, count)[: count * (2 * count - 1)]
    upper = repeated.reshape(count, 2 * count - 1)[:, :count]
    matrix = upper.T + jnp.eye(count, dtype=filter_taps.dtype)
    return matrix.astype(jnp.bfloat16)


def is_power_of_two(count):
    return count > 0 and count & (count - 1) == 0


def swap(block, axis, count, bit):
    return lax.ppermute(block, axis, [(i, i ^ bit) for i in range(count)])


def tree_sum(block, axis):
    count = lax.axis_size(axis)
    if not is_power_of_two(count):
        return lax.psum(block, axis)
    bit = 1
    while bit < count:
        block = block + swap(block, axis, count, bit)
        bit *= 2
    return block


def tree_sum_under(block, axis, pieces):
    count = lax.axis_size(axis)
    bit = 1
    while bit < count:
        arrived = swap(block, axis, count, bit)
        arrived, _ = lax.optimization_barrier((arrived, pieces.pop(0)()))
        block = block + arrived
        bit *= 2
    return block


def shift_sum(block, axis):
    count = lax.axis_size(axis)
    arrived = [
        lax.ppermute(block, axis, [(i, (i + shift) % count) for i in range(count)])
        for shift in range(1, count)
    ]
    for other in arrived:
        block = block + other
    return block


def tree_broadcast(block, fold_ratio, companion, on_first=None):
    row_count = lax.axis_size("row")
    col_count = lax.axis_size("col")
    owner = lax.axis_index("row") // fold_ratio
    offset = lax.axis_index("col") ^ owner
    if not is_power_of_two(col_count):
        block = jnp.where(offset == 0, block, jnp.zeros_like(block))
        return lax.psum(block, "col"), companion()
    bits = [1 << k for k in range(1, col_count.bit_length() - 1)] + [1][: col_count > 1]
    done = 0
    for bit in bits:
        pairs = []
        for row in range(row_count):
            base = row * col_count
            row_owner = row // fold_ratio
            for held in range(col_count):
                if (held ^ row_owner) & ~done == 0:
                    pairs.append((base + held, base + (held ^ bit)))
        arrived = lax.ppermute(block, ("row", "col"), pairs)
        done |= bit
        block = jnp.where((offset & ~done == 0) & (offset & bit != 0), arrived, block)
        block, companion = lax.optimization_barrier((block, companion()))
        companion = lambda held=companion: held
        if on_first is not None:
            block = on_first(block)
            on_first = None
    return block, companion()


def product_kernel(left_ref, right_ref, out_ref):
    out_ref[...] = lax.dot_general(
        left_ref[...], right_ref[...], (((0,), (0,)), ((), ())), preferred_element_type=jnp.float32
    )


def normal_rows(left, right, total_rows, first_row, previous):
    epochs, rows = left.shape
    width = right.shape[1]
    tile_rows = 512 if rows % 512 == 0 else rows
    tile_cols = 2048 if width % 2048 == 0 else width
    row_offset = first_row // tile_rows
    in_specs = [
        pl.BlockSpec((epochs, tile_rows), lambda j, i: (0, i)),
        pl.BlockSpec((epochs, tile_cols), lambda j, i: (0, j)),
    ]
    operands = [left, right]
    aliases = {}
    if previous is not None:
        in_specs.append(pl.BlockSpec(memory_space=pl.ANY))
        operands.append(previous)
        aliases = {2: 0}

    def kernel(left_ref, right_ref, *rest):
        product_kernel(left_ref, right_ref, rest[-1])

    return pl.pallas_call(
        kernel,
        grid=(width // tile_cols, rows // tile_rows),
        in_specs=in_specs,
        out_specs=pl.BlockSpec((tile_rows, tile_cols), lambda j, i: (i + row_offset, j)),
        out_shape=jax.ShapeDtypeStruct((total_rows, width), jnp.float32),
        input_output_aliases=aliases,
        compiler_params=pltpu.CompilerParams(vmem_limit_bytes=48 * 1024 * 1024),
        cost_estimate=pl.CostEstimate(
            flops=2 * rows * epochs * width,
            transcendentals=0,
            bytes_accessed=rows * width * 4 + epochs * width * 2 + rows * epochs * 2,
        ),
    )(*operands)


def contract_epochs(left, right):
    return lax.dot_general(
        left, right, (((0,), (0,)), ((), ())), precision=lax.Precision.HIGH
    )


def body(design, filter_taps, probes, lower_bound, upper_bound):
    row_count = lax.axis_size("row")
    col_count = lax.axis_size("col")
    fold_ratio = row_count // col_count
    row_index = lax.axis_index("row")
    panel_width = design.shape[1]
    row_width = panel_width // fold_ratio
    filter_matrix = whitening(filter_taps)
    whole_panel = lax.all_gather(design, "row", axis=0, tiled=True)
    white = jnp.dot(filter_matrix, whole_panel, preferred_element_type=jnp.float32).astype(
        jnp.bfloat16
    )
    own_slice = lax.dynamic_slice_in_dim(white, row_index % fold_ratio * row_width, row_width, 1)

    def couple():
        white_wide = held["white"].astype(jnp.float32)
        panel_jacobi = jnp.sum(jnp.square(white_wide), axis=0) + 1e-06
        coupling = jnp.dot(
            white_wide / panel_jacobi[None, :], white_wide.T, precision=lax.Precision.HIGH
        )
        return tree_sum(coupling, "col")

    half_rows = row_width // 2
    held = {}

    def release_second(block):
        held["second"], held["white"], block = lax.optimization_barrier(
            (own_slice[:, half_rows:], white, block)
        )
        return block

    panel_first, _ = tree_broadcast(
        own_slice[:, :half_rows], fold_ratio, lambda: (), release_second
    )
    coupling = couple()
    panel_second, normal_tile = tree_broadcast(
        held["second"],
        fold_ratio,
        lambda: normal_rows(panel_first, white, row_width, 0, None),
    )
    panel = jnp.concatenate([panel_first, panel_second], axis=1)
    panel_wide = panel.astype(jnp.float32)
    jacobi = (jnp.sum(jnp.square(panel_wide), axis=0) + 1e-06)[:, None]
    center_value = (lower_bound[0] + upper_bound[0]) / 2.0
    half_width = (upper_bound[0] - lower_bound[0]) / 2.0
    sigma_value = center_value / half_width
    weight_now = 1.0 / sigma_value
    residual = probes
    scaled = residual / jacobi
    direction = scaled / center_value
    partial_image = jnp.dot(panel_wide, scaled, precision=lax.Precision.HIGH)
    if is_power_of_two(row_count) and row_count > 1:
        step_count = row_count.bit_length() - 1
        piece_rows = half_rows // step_count
        tile = {"normal": normal_tile}

        def piece(index):
            def run():
                start = index * piece_rows
                stop = half_rows if index == step_count - 1 else start + piece_rows
                tile["normal"] = normal_rows(
                    panel_second[:, start:stop], white, row_width, half_rows + start, tile["normal"]
                )
                return tile["normal"]

            return run

        scaled_image = tree_sum_under(partial_image, "row", [piece(i) for i in range(step_count)])
        normal_tile = tile["normal"]
    else:
        normal_tile = normal_rows(panel_second, white, row_width, half_rows, normal_tile)
        scaled_image = tree_sum(partial_image, "row")
    image = scaled_image / center_value
    solution = jnp.zeros_like(residual)
    for sweep_index in range(SWEEPS):
        solution = solution + direction
        residual = residual - contract_epochs(panel_wide, image)
        weight_next = 1.0 / (2.0 * sigma_value - weight_now)
        direction = weight_next * weight_now * direction + 2.0 * weight_next / half_width * (
            residual / jacobi
        )
        if sweep_index + 1 < SWEEPS:
            scaled_image = scaled_image - jnp.dot(
                coupling, image, precision=lax.Precision.HIGH
            )
            image = weight_next * weight_now * image + 2.0 * weight_next / half_width * scaled_image
        weight_now = weight_next
    solution = solution + direction
    return (normal_tile, solution)


def solution(mesh):
    placed = (P("row", "col"), P(), P("row", "col"), P(), P())
    return jax.shard_map(
        body,
        mesh=mesh,
        in_specs=placed,
        out_specs=(P("row", "col"), P("row", "col")),
        check_vma=False,
    )
```

```python
import jax
import jax.numpy as jnp
from jax import lax
from jax.experimental import pallas as pl
from jax.experimental.pallas import tpu as pltpu
from jax.sharding import PartitionSpec as P

SWEEPS = 2


def whitening(filter_taps):
    count = filter_taps.shape[0]
    padded = jnp.concatenate([filter_taps, jnp.zeros_like(filter_taps)])
    repeated = jnp.tile(padded, count)[: count * (2 * count - 1)]
    upper = repeated.reshape(count, 2 * count - 1)[:, :count]
    matrix = upper.T + jnp.eye(count, dtype=filter_taps.dtype)
    return matrix.astype(jnp.bfloat16)


def is_power_of_two(count):
    return count > 0 and count & (count - 1) == 0


def swap(block, axis, count, bit):
    return lax.ppermute(block, axis, [(i, i ^ bit) for i in range(count)])


def tree_sum(block, axis):
    count = lax.axis_size(axis)
    if not is_power_of_two(count):
        return lax.psum(block, axis)
    bit = 1
    while bit < count:
        block = block + swap(block, axis, count, bit)
        bit *= 2
    return block


def shift_sum(block, axis):
    count = lax.axis_size(axis)
    arrived = [
        lax.ppermute(block, axis, [(i, (i + shift) % count) for i in range(count)])
        for shift in range(1, count)
    ]
    for other in arrived:
        block = block + other
    return block


def tree_broadcast(block, fold_ratio, companion, on_first=None):
    row_count = lax.axis_size("row")
    col_count = lax.axis_size("col")
    owner = lax.axis_index("row") // fold_ratio
    offset = lax.axis_index("col") ^ owner
    if not is_power_of_two(col_count):
        block = jnp.where(offset == 0, block, jnp.zeros_like(block))
        return lax.psum(block, "col"), companion()
    bits = [1 << k for k in range(1, col_count.bit_length() - 1)] + [1][: col_count > 1]
    done = 0
    for bit in bits:
        pairs = []
        for row in range(row_count):
            base = row * col_count
            row_owner = row // fold_ratio
            for held in range(col_count):
                if (held ^ row_owner) & ~done == 0:
                    pairs.append((base + held, base + (held ^ bit)))
        arrived = lax.ppermute(block, ("row", "col"), pairs)
        done |= bit
        block = jnp.where((offset & ~done == 0) & (offset & bit != 0), arrived, block)
        block, companion = lax.optimization_barrier((block, companion()))
        companion = lambda held=companion: held
        if on_first is not None:
            block = on_first(block)
            on_first = None
    return block, companion()


def product_kernel(left_ref, right_ref, out_ref):
    out_ref[...] = lax.dot_general(
        left_ref[...], right_ref[...], (((0,), (0,)), ((), ())), preferred_element_type=jnp.float32
    )


def normal_rows(left, right, total_rows, first_row, previous):
    epochs, rows = left.shape
    width = right.shape[1]
    tile_rows = 512 if rows % 512 == 0 else rows
    tile_cols = 2048 if width % 2048 == 0 else width
    row_offset = first_row // tile_rows
    in_specs = [
        pl.BlockSpec((epochs, tile_rows), lambda j, i: (0, i)),
        pl.BlockSpec((epochs, tile_cols), lambda j, i: (0, j)),
    ]
    operands = [left, right]
    aliases = {}
    if previous is not None:
        in_specs.append(pl.BlockSpec(memory_space=pl.ANY))
        operands.append(previous)
        aliases = {2: 0}

    def kernel(left_ref, right_ref, *rest):
        product_kernel(left_ref, right_ref, rest[-1])

    return pl.pallas_call(
        kernel,
        grid=(width // tile_cols, rows // tile_rows),
        in_specs=in_specs,
        out_specs=pl.BlockSpec((tile_rows, tile_cols), lambda j, i: (i + row_offset, j)),
        out_shape=jax.ShapeDtypeStruct((total_rows, width), jnp.float32),
        input_output_aliases=aliases,
        compiler_params=pltpu.CompilerParams(vmem_limit_bytes=48 * 1024 * 1024),
        cost_estimate=pl.CostEstimate(
            flops=2 * rows * epochs * width,
            transcendentals=0,
            bytes_accessed=rows * width * 4 + epochs * width * 2 + rows * epochs * 2,
        ),
    )(*operands)


def contract_epochs(left, right):
    return lax.dot_general(
        left, right, (((0,), (0,)), ((), ())), precision=lax.Precision.HIGH
    )


def body(design, filter_taps, probes, lower_bound, upper_bound):
    row_count = lax.axis_size("row")
    col_count = lax.axis_size("col")
    fold_ratio = row_count // col_count
    row_index = lax.axis_index("row")
    panel_width = design.shape[1]
    row_width = panel_width // fold_ratio
    filter_matrix = whitening(filter_taps)
    whole_panel = lax.all_gather(design, "row", axis=0, tiled=True)
    white = jnp.dot(filter_matrix, whole_panel, preferred_element_type=jnp.float32).astype(
        jnp.bfloat16
    )
    first_column = row_index % fold_ratio * row_width
    half_rows = row_width // 2

    def whiten_rows(start):
        block = lax.dynamic_slice_in_dim(whole_panel, first_column + start, half_rows, 1)
        return jnp.dot(filter_matrix, block, preferred_element_type=jnp.float32).astype(jnp.bfloat16)


    def couple():
        white_wide = held["white"].astype(jnp.float32)
        panel_jacobi = jnp.sum(jnp.square(white_wide), axis=0) + 1e-06
        coupling = jnp.dot(
            white_wide / panel_jacobi[None, :], white_wide.T, precision=lax.Precision.HIGH
        )
        return tree_sum(coupling, "col")

    held = {}

    def release_second(block):
        held["second"], held["white"], block = lax.optimization_barrier(
            (whiten_rows(half_rows), white, block)
        )
        return block

    panel_first, _ = tree_broadcast(
        whiten_rows(0), fold_ratio, lambda: (), release_second
    )
    coupling = couple()
    panel_second, normal_tile = tree_broadcast(
        held["second"],
        fold_ratio,
        lambda: normal_rows(panel_first, white, row_width, 0, None),
    )
    normal_tile = normal_rows(panel_second, white, row_width, half_rows, normal_tile)
    panel = jnp.concatenate([panel_first, panel_second], axis=1)
    panel_wide = panel.astype(jnp.float32)
    jacobi = (jnp.sum(jnp.square(panel_wide), axis=0) + 1e-06)[:, None]
    center_value = (lower_bound[0] + upper_bound[0]) / 2.0
    half_width = (upper_bound[0] - lower_bound[0]) / 2.0
    sigma_value = center_value / half_width
    weight_now = 1.0 / sigma_value
    residual = probes
    scaled = residual / jacobi
    direction = scaled / center_value
    scaled_image = tree_sum(jnp.dot(panel_wide, scaled, precision=lax.Precision.HIGH), "row")
    image = scaled_image / center_value
    solution = jnp.zeros_like(residual)
    for sweep_index in range(SWEEPS):
        solution = solution + direction
        residual = residual - contract_epochs(panel_wide, image)
        weight_next = 1.0 / (2.0 * sigma_value - weight_now)
        direction = weight_next * weight_now * direction + 2.0 * weight_next / half_width * (
            residual / jacobi
        )
        if sweep_index + 1 < SWEEPS:
            scaled_image = scaled_image - jnp.dot(
                coupling, image, precision=lax.Precision.HIGH
            )
            image = weight_next * weight_now * image + 2.0 * weight_next / half_width * scaled_image
        weight_now = weight_next
    solution = solution + direction
    return (normal_tile, solution)


def solution(mesh):
    placed = (P("row", "col"), P(), P("row", "col"), P(), P())
    return jax.shard_map(
        body,
        mesh=mesh,
        in_specs=placed,
        out_specs=(P("row", "col"), P("row", "col")),
        check_vma=False,
    )
```

```python
import jax
import jax.numpy as jnp
from jax import lax
from jax.experimental import pallas as pl
from jax.experimental.pallas import tpu as pltpu
from jax.sharding import PartitionSpec as P

SWEEPS = 2


def whitening(filter_taps):
    count = filter_taps.shape[0]
    padded = jnp.concatenate([filter_taps, jnp.zeros_like(filter_taps)])
    repeated = jnp.tile(padded, count)[: count * (2 * count - 1)]
    upper = repeated.reshape(count, 2 * count - 1)[:, :count]
    matrix = upper.T + jnp.eye(count, dtype=filter_taps.dtype)
    return matrix.astype(jnp.bfloat16)


def is_power_of_two(count):
    return count > 0 and count & (count - 1) == 0


def swap(block, axis, count, bit):
    return lax.ppermute(block, axis, [(i, i ^ bit) for i in range(count)])


def tree_sum(block, axis):
    count = lax.axis_size(axis)
    if not is_power_of_two(count):
        return lax.psum(block, axis)
    bit = 1
    while bit < count:
        block = block + swap(block, axis, count, bit)
        bit *= 2
    return block


def tree_gather(block, axis):
    count = lax.axis_size(axis)
    if not is_power_of_two(count):
        return lax.all_gather(block, axis, axis=0, tiled=True)
    index = lax.axis_index(axis)
    bit = 1
    while bit < count:
        other = swap(block, axis, count, bit)
        block = jnp.where(
            index & bit == 0,
            jnp.concatenate([block, other], axis=0),
            jnp.concatenate([other, block], axis=0),
        )
        bit *= 2
    return block


def shift_sum(block, axis):
    count = lax.axis_size(axis)
    arrived = [
        lax.ppermute(block, axis, [(i, (i + shift) % count) for i in range(count)])
        for shift in range(1, count)
    ]
    for other in arrived:
        block = block + other
    return block


def tree_broadcast(block, fold_ratio, companion, on_first=None):
    row_count = lax.axis_size("row")
    col_count = lax.axis_size("col")
    owner = lax.axis_index("row") // fold_ratio
    offset = lax.axis_index("col") ^ owner
    if not is_power_of_two(col_count):
        block = jnp.where(offset == 0, block, jnp.zeros_like(block))
        return lax.psum(block, "col"), companion()
    bits = [1 << k for k in range(1, col_count.bit_length() - 1)] + [1][: col_count > 1]
    done = 0
    for bit in bits:
        pairs = []
        for row in range(row_count):
            base = row * col_count
            row_owner = row // fold_ratio
            for held in range(col_count):
                if (held ^ row_owner) & ~done == 0:
                    pairs.append((base + held, base + (held ^ bit)))
        arrived = lax.ppermute(block, ("row", "col"), pairs)
        done |= bit
        block = jnp.where((offset & ~done == 0) & (offset & bit != 0), arrived, block)
        block, companion = lax.optimization_barrier((block, companion()))
        companion = lambda held=companion: held
        if on_first is not None:
            block = on_first(block)
            on_first = None
    return block, companion()


def product_kernel(left_ref, right_ref, out_ref):
    out_ref[...] = lax.dot_general(
        left_ref[...], right_ref[...], (((0,), (0,)), ((), ())), preferred_element_type=jnp.float32
    )


def normal_rows(left, right, total_rows, first_row, previous):
    epochs, rows = left.shape
    width = right.shape[1]
    tile_rows = 512 if rows % 512 == 0 else rows
    tile_cols = 2048 if width % 2048 == 0 else width
    row_offset = first_row // tile_rows
    in_specs = [
        pl.BlockSpec((epochs, tile_rows), lambda j, i: (0, i)),
        pl.BlockSpec((epochs, tile_cols), lambda j, i: (0, j)),
    ]
    operands = [left, right]
    aliases = {}
    if previous is not None:
        in_specs.append(pl.BlockSpec(memory_space=pl.ANY))
        operands.append(previous)
        aliases = {2: 0}

    def kernel(left_ref, right_ref, *rest):
        product_kernel(left_ref, right_ref, rest[-1])

    return pl.pallas_call(
        kernel,
        grid=(width // tile_cols, rows // tile_rows),
        in_specs=in_specs,
        out_specs=pl.BlockSpec((tile_rows, tile_cols), lambda j, i: (i + row_offset, j)),
        out_shape=jax.ShapeDtypeStruct((total_rows, width), jnp.float32),
        input_output_aliases=aliases,
        compiler_params=pltpu.CompilerParams(vmem_limit_bytes=48 * 1024 * 1024),
        cost_estimate=pl.CostEstimate(
            flops=2 * rows * epochs * width,
            transcendentals=0,
            bytes_accessed=rows * width * 4 + epochs * width * 2 + rows * epochs * 2,
        ),
    )(*operands)


def contract_epochs(left, right):
    return lax.dot_general(
        left, right, (((0,), (0,)), ((), ())), precision=lax.Precision.HIGH
    )


def body(design, filter_taps, probes, lower_bound, upper_bound):
    row_count = lax.axis_size("row")
    col_count = lax.axis_size("col")
    fold_ratio = row_count // col_count
    row_index = lax.axis_index("row")
    panel_width = design.shape[1]
    row_width = panel_width // fold_ratio
    filter_matrix = whitening(filter_taps)
    offloaded = panel_width * 2 // 3 // 128 * 128
    whole_panel = jnp.concatenate(
        [
            lax.all_gather(design[:, :offloaded], "row", axis=0, tiled=True),
            tree_gather(design[:, offloaded:], "row"),
        ],
        axis=1,
    )
    white = jnp.dot(filter_matrix, whole_panel, preferred_element_type=jnp.float32).astype(
        jnp.bfloat16
    )
    first_column = row_index % fold_ratio * row_width
    half_rows = row_width // 2

    def whiten_rows(start):
        block = lax.dynamic_slice_in_dim(whole_panel, first_column + start, half_rows, 1)
        return jnp.dot(filter_matrix, block, preferred_element_type=jnp.float32).astype(jnp.bfloat16)


    def couple():
        white_wide = held["white"].astype(jnp.float32)
        panel_jacobi = jnp.sum(jnp.square(white_wide), axis=0) + 1e-06
        coupling = jnp.dot(
            white_wide / panel_jacobi[None, :], white_wide.T, precision=lax.Precision.HIGH
        )
        return tree_sum(coupling, "col")

    held = {}

    def release_second(block):
        held["second"], held["white"], block = lax.optimization_barrier(
            (whiten_rows(half_rows), white, block)
        )
        return block

    panel_first, _ = tree_broadcast(
        whiten_rows(0), fold_ratio, lambda: (), release_second
    )
    coupling = couple()
    panel_second, normal_tile = tree_broadcast(
        held["second"],
        fold_ratio,
        lambda: normal_rows(panel_first, white, row_width, 0, None),
    )
    normal_tile = normal_rows(panel_second, white, row_width, half_rows, normal_tile)
    panel = jnp.concatenate([panel_first, panel_second], axis=1)
    panel_wide = panel.astype(jnp.float32)
    jacobi = (jnp.sum(jnp.square(panel_wide), axis=0) + 1e-06)[:, None]
    center_value = (lower_bound[0] + upper_bound[0]) / 2.0
    half_width = (upper_bound[0] - lower_bound[0]) / 2.0
    sigma_value = center_value / half_width
    weight_now = 1.0 / sigma_value
    residual = probes
    scaled = residual / jacobi
    direction = scaled / center_value
    scaled_image = tree_sum(jnp.dot(panel_wide, scaled, precision=lax.Precision.HIGH), "row")
    image = scaled_image / center_value
    solution = jnp.zeros_like(residual)
    for sweep_index in range(SWEEPS):
        solution = solution + direction
        residual = residual - contract_epochs(panel_wide, image)
        weight_next = 1.0 / (2.0 * sigma_value - weight_now)
        direction = weight_next * weight_now * direction + 2.0 * weight_next / half_width * (
            residual / jacobi
        )
        if sweep_index + 1 < SWEEPS:
            scaled_image = scaled_image - jnp.dot(
                coupling, image, precision=lax.Precision.HIGH
            )
            image = weight_next * weight_now * image + 2.0 * weight_next / half_width * scaled_image
        weight_now = weight_next
    solution = solution + direction
    return (normal_tile, solution)


def solution(mesh):
    placed = (P("row", "col"), P(), P("row", "col"), P(), P())
    return jax.shard_map(
        body,
        mesh=mesh,
        in_specs=placed,
        out_specs=(P("row", "col"), P("row", "col")),
        check_vma=False,
    )
```

```python
import jax
import jax.numpy as jnp
from jax import lax
from jax.experimental import pallas as pl
from jax.experimental.pallas import tpu as pltpu
from jax.sharding import PartitionSpec as P

SWEEPS = 2


def whitening(filter_taps):
    count = filter_taps.shape[0]
    padded = jnp.concatenate([filter_taps, jnp.zeros_like(filter_taps)])
    repeated = jnp.tile(padded, count)[: count * (2 * count - 1)]
    upper = repeated.reshape(count, 2 * count - 1)[:, :count]
    matrix = upper.T + jnp.eye(count, dtype=filter_taps.dtype)
    return matrix.astype(jnp.bfloat16)


def is_power_of_two(count):
    return count > 0 and count & (count - 1) == 0


def swap(block, axis, count, bit):
    return lax.ppermute(block, axis, [(i, i ^ bit) for i in range(count)])


def tree_sum(block, axis):
    count = lax.axis_size(axis)
    if not is_power_of_two(count):
        return lax.psum(block, axis)
    bit = 1
    while bit < count:
        block = block + swap(block, axis, count, bit)
        bit *= 2
    return block


def shift_sum(block, axis):
    count = lax.axis_size(axis)
    arrived = [
        lax.ppermute(block, axis, [(i, (i + shift) % count) for i in range(count)])
        for shift in range(1, count)
    ]
    for other in arrived:
        block = block + other
    return block


def tree_broadcast(block, fold_ratio, companion, on_first=None):
    row_count = lax.axis_size("row")
    col_count = lax.axis_size("col")
    owner = lax.axis_index("row") // fold_ratio
    offset = lax.axis_index("col") ^ owner
    if not is_power_of_two(col_count):
        block = jnp.where(offset == 0, block, jnp.zeros_like(block))
        return lax.psum(block, "col"), companion()
    bits = [1 << k for k in range(1, col_count.bit_length() - 1)] + [1][: col_count > 1]
    done = 0
    for bit in bits:
        pairs = []
        for row in range(row_count):
            base = row * col_count
            row_owner = row // fold_ratio
            for held in range(col_count):
                if (held ^ row_owner) & ~done == 0:
                    pairs.append((base + held, base + (held ^ bit)))
        arrived = lax.ppermute(block, ("row", "col"), pairs)
        done |= bit
        block = jnp.where((offset & ~done == 0) & (offset & bit != 0), arrived, block)
        block, companion = lax.optimization_barrier((block, companion()))
        companion = lambda held=companion: held
        if on_first is not None:
            block = on_first(block)
            on_first = None
    return block, companion()


def product_kernel(left_ref, right_ref, out_ref):
    out_ref[...] = lax.dot_general(
        left_ref[...], right_ref[...], (((0,), (0,)), ((), ())), preferred_element_type=jnp.float32
    )


def normal_rows(left, right, total_rows, first_row, previous):
    epochs, rows = left.shape
    width = right.shape[1]
    tile_rows = 256 if rows % 256 == 0 else rows
    tile_cols = width
    row_offset = first_row // tile_rows
    in_specs = [
        pl.BlockSpec((epochs, tile_rows), lambda j, i: (0, i)),
        pl.BlockSpec((epochs, tile_cols), lambda j, i: (0, j)),
    ]
    operands = [left, right]
    aliases = {}
    if previous is not None:
        in_specs.append(pl.BlockSpec(memory_space=pl.ANY))
        operands.append(previous)
        aliases = {2: 0}

    def kernel(left_ref, right_ref, *rest):
        product_kernel(left_ref, right_ref, rest[-1])

    return pl.pallas_call(
        kernel,
        grid=(width // tile_cols, rows // tile_rows),
        in_specs=in_specs,
        out_specs=pl.BlockSpec((tile_rows, tile_cols), lambda j, i: (i + row_offset, j)),
        out_shape=jax.ShapeDtypeStruct((total_rows, width), jnp.float32),
        input_output_aliases=aliases,
        compiler_params=pltpu.CompilerParams(vmem_limit_bytes=48 * 1024 * 1024),
        cost_estimate=pl.CostEstimate(
            flops=2 * rows * epochs * width,
            transcendentals=0,
            bytes_accessed=rows * width * 4 + epochs * width * 2 + rows * epochs * 2,
        ),
    )(*operands)


def contract_epochs(left, right):
    return lax.dot_general(
        left, right, (((0,), (0,)), ((), ())), precision=lax.Precision.HIGH
    )


def body(design, filter_taps, probes, lower_bound, upper_bound):
    row_count = lax.axis_size("row")
    col_count = lax.axis_size("col")
    fold_ratio = row_count // col_count
    row_index = lax.axis_index("row")
    panel_width = design.shape[1]
    row_width = panel_width // fold_ratio
    filter_matrix = whitening(filter_taps)
    whole_panel = lax.all_gather(design, "row", axis=0, tiled=True)
    white = jnp.dot(filter_matrix, whole_panel, preferred_element_type=jnp.float32).astype(
        jnp.bfloat16
    )
    first_column = row_index % fold_ratio * row_width
    half_rows = row_width // 2

    def whiten_rows(start):
        block = lax.dynamic_slice_in_dim(whole_panel, first_column + start, half_rows, 1)
        return jnp.dot(filter_matrix, block, preferred_element_type=jnp.float32).astype(jnp.bfloat16)


    def couple():
        white_wide = held["white"].astype(jnp.float32)
        panel_jacobi = jnp.sum(jnp.square(white_wide), axis=0) + 1e-06
        coupling = jnp.dot(
            white_wide / panel_jacobi[None, :], white_wide.T, precision=lax.Precision.HIGH
        )
        return tree_sum(coupling, "col")

    held = {}

    def release_second(block):
        held["second"], held["white"], block = lax.optimization_barrier(
            (whiten_rows(half_rows), white, block)
        )
        return block

    panel_first, _ = tree_broadcast(
        whiten_rows(0), fold_ratio, lambda: (), release_second
    )
    coupling = couple()
    panel_second, normal_tile = tree_broadcast(
        held["second"],
        fold_ratio,
        lambda: normal_rows(panel_first, white, row_width, 0, None),
    )
    normal_tile = normal_rows(panel_second, white, row_width, half_rows, normal_tile)
    panel = jnp.concatenate([panel_first, panel_second], axis=1)
    panel_wide = panel.astype(jnp.float32)
    jacobi = (jnp.sum(jnp.square(panel_wide), axis=0) + 1e-06)[:, None]
    center_value = (lower_bound[0] + upper_bound[0]) / 2.0
    half_width = (upper_bound[0] - lower_bound[0]) / 2.0
    sigma_value = center_value / half_width
    weight_now = 1.0 / sigma_value
    residual = probes
    scaled = residual / jacobi
    direction = scaled / center_value
    scaled_image = tree_sum(jnp.dot(panel_wide, scaled, precision=lax.Precision.HIGH), "row")
    image = scaled_image / center_value
    solution = jnp.zeros_like(residual)
    for sweep_index in range(SWEEPS):
        solution = solution + direction
        residual = residual - contract_epochs(panel_wide, image)
        weight_next = 1.0 / (2.0 * sigma_value - weight_now)
        direction = weight_next * weight_now * direction + 2.0 * weight_next / half_width * (
            residual / jacobi
        )
        if sweep_index + 1 < SWEEPS:
            scaled_image = scaled_image - jnp.dot(
                coupling, image, precision=lax.Precision.HIGH
            )
            image = weight_next * weight_now * image + 2.0 * weight_next / half_width * scaled_image
        weight_now = weight_next
    solution = solution + direction
    return (normal_tile, solution)


def solution(mesh):
    placed = (P("row", "col"), P(), P("row", "col"), P(), P())
    return jax.shard_map(
        body,
        mesh=mesh,
        in_specs=placed,
        out_specs=(P("row", "col"), P("row", "col")),
        check_vma=False,
    )
```

```python
import jax
import jax.numpy as jnp
from jax import lax
from jax.experimental import pallas as pl
from jax.experimental.pallas import tpu as pltpu
from jax.sharding import PartitionSpec as P

SWEEPS = 2


def whitening(filter_taps):
    count = filter_taps.shape[0]
    padded = jnp.concatenate([filter_taps, jnp.zeros_like(filter_taps)])
    repeated = jnp.tile(padded, count)[: count * (2 * count - 1)]
    upper = repeated.reshape(count, 2 * count - 1)[:, :count]
    matrix = upper.T + jnp.eye(count, dtype=filter_taps.dtype)
    return matrix.astype(jnp.bfloat16)


def is_power_of_two(count):
    return count > 0 and count & (count - 1) == 0


def swap(block, axis, count, bit):
    return lax.ppermute(block, axis, [(i, i ^ bit) for i in range(count)])


def tree_sum(block, axis):
    count = lax.axis_size(axis)
    if not is_power_of_two(count):
        return lax.psum(block, axis)
    bit = 1
    while bit < count:
        block = block + swap(block, axis, count, bit)
        bit *= 2
    return block


def shift_sum(block, axis):
    count = lax.axis_size(axis)
    arrived = [
        lax.ppermute(block, axis, [(i, (i + shift) % count) for i in range(count)])
        for shift in range(1, count)
    ]
    for other in arrived:
        block = block + other
    return block


def tree_broadcast(block, fold_ratio, companion, on_first=None):
    row_count = lax.axis_size("row")
    col_count = lax.axis_size("col")
    owner = lax.axis_index("row") // fold_ratio
    offset = lax.axis_index("col") ^ owner
    if not is_power_of_two(col_count):
        block = jnp.where(offset == 0, block, jnp.zeros_like(block))
        return lax.psum(block, "col"), companion()
    bits = [1 << k for k in range(1, col_count.bit_length() - 1)] + [1][: col_count > 1]
    done = 0
    for bit in bits:
        pairs = []
        for row in range(row_count):
            base = row * col_count
            row_owner = row // fold_ratio
            for held in range(col_count):
                if (held ^ row_owner) & ~done == 0:
                    pairs.append((base + held, base + (held ^ bit)))
        arrived = lax.ppermute(block, ("row", "col"), pairs)
        done |= bit
        block = jnp.where((offset & ~done == 0) & (offset & bit != 0), arrived, block)
        block, companion = lax.optimization_barrier((block, companion()))
        companion = lambda held=companion: held
        if on_first is not None:
            block = on_first(block)
            on_first = None
    return block, companion()


def product_kernel(left_ref, right_ref, out_ref):
    out_ref[...] = lax.dot_general(
        left_ref[...], right_ref[...], (((0,), (0,)), ((), ())), preferred_element_type=jnp.float32
    )


def normal_rows(left, right, total_rows, first_row, previous):
    epochs, rows = left.shape
    width = right.shape[1]
    tile_rows = 512 if rows % 512 == 0 else rows
    tile_cols = width
    row_offset = first_row // tile_rows
    in_specs = [
        pl.BlockSpec((epochs, tile_rows), lambda j, i: (0, i)),
        pl.BlockSpec((epochs, tile_cols), lambda j, i: (0, j)),
    ]
    operands = [left, right]
    aliases = {}
    if previous is not None:
        in_specs.append(pl.BlockSpec(memory_space=pl.ANY))
        operands.append(previous)
        aliases = {2: 0}

    def kernel(left_ref, right_ref, *rest):
        product_kernel(left_ref, right_ref, rest[-1])

    return pl.pallas_call(
        kernel,
        grid=(width // tile_cols, rows // tile_rows),
        in_specs=in_specs,
        out_specs=pl.BlockSpec((tile_rows, tile_cols), lambda j, i: (i + row_offset, j)),
        out_shape=jax.ShapeDtypeStruct((total_rows, width), jnp.float32),
        input_output_aliases=aliases,
        compiler_params=pltpu.CompilerParams(vmem_limit_bytes=48 * 1024 * 1024),
        cost_estimate=pl.CostEstimate(
            flops=2 * rows * epochs * width,
            transcendentals=0,
            bytes_accessed=rows * width * 4 + epochs * width * 2 + rows * epochs * 2,
        ),
    )(*operands)


def contract_epochs(left, right):
    return lax.dot_general(
        left, right, (((0,), (0,)), ((), ())), precision=lax.Precision.HIGH
    )


def body(design, filter_taps, probes, lower_bound, upper_bound):
    row_count = lax.axis_size("row")
    col_count = lax.axis_size("col")
    fold_ratio = row_count // col_count
    row_index = lax.axis_index("row")
    panel_width = design.shape[1]
    row_width = panel_width // fold_ratio
    filter_matrix = whitening(filter_taps)
    whole_panel = lax.all_gather(design, "row", axis=0, tiled=True)
    white = jnp.dot(filter_matrix, whole_panel, preferred_element_type=jnp.float32).astype(
        jnp.bfloat16
    )
    first_column = row_index % fold_ratio * row_width
    half_rows = row_width // 2

    def whiten_rows(start):
        block = lax.dynamic_slice_in_dim(whole_panel, first_column + start, half_rows, 1)
        return jnp.dot(filter_matrix, block, preferred_element_type=jnp.float32).astype(jnp.bfloat16)


    def couple():
        white_wide = held["white"].astype(jnp.float32)
        panel_jacobi = jnp.sum(jnp.square(white_wide), axis=0) + 1e-06
        coupling = jnp.dot(
            white_wide / panel_jacobi[None, :], white_wide.T, precision=lax.Precision.HIGH
        )
        return tree_sum(coupling, "col")

    held = {}

    def release_second(block):
        held["second"], held["white"], block = lax.optimization_barrier(
            (whiten_rows(half_rows), white, block)
        )
        return block

    panel_first, _ = tree_broadcast(
        whiten_rows(0), fold_ratio, lambda: (), release_second
    )
    coupling = couple()
    panel_second, normal_tile = tree_broadcast(
        held["second"],
        fold_ratio,
        lambda: normal_rows(panel_first, white, row_width, 0, None),
    )
    normal_tile = normal_rows(panel_second, white, row_width, half_rows, normal_tile)
    panel = jnp.concatenate([panel_first, panel_second], axis=1)
    panel_wide = panel.astype(jnp.float32)
    jacobi = (jnp.sum(jnp.square(panel_wide), axis=0) + 1e-06)[:, None]
    center_value = (lower_bound[0] + upper_bound[0]) / 2.0
    half_width = (upper_bound[0] - lower_bound[0]) / 2.0
    sigma_value = center_value / half_width
    weight_now = 1.0 / sigma_value
    residual = probes
    scaled = residual / jacobi
    direction = scaled / center_value
    scaled_image = tree_sum(jnp.dot(panel_wide, scaled, precision=lax.Precision.HIGH), "row")
    image = scaled_image / center_value
    solution = jnp.zeros_like(residual)
    for sweep_index in range(SWEEPS):
        solution = solution + direction
        residual = residual - contract_epochs(panel_wide, image)
        weight_next = 1.0 / (2.0 * sigma_value - weight_now)
        direction = weight_next * weight_now * direction + 2.0 * weight_next / half_width * (
            residual / jacobi
        )
        if sweep_index + 1 < SWEEPS:
            scaled_image = scaled_image - jnp.dot(
                coupling, image, precision=lax.Precision.HIGH
            )
            image = weight_next * weight_now * image + 2.0 * weight_next / half_width * scaled_image
        weight_now = weight_next
    solution = solution + direction
    return (normal_tile, solution)


def solution(mesh):
    placed = (P("row", "col"), P(), P("row", "col"), P(), P())
    return jax.shard_map(
        body,
        mesh=mesh,
        in_specs=placed,
        out_specs=(P("row", "col"), P("row", "col")),
        check_vma=False,
    )
```

```python
import jax
import jax.numpy as jnp
from jax import lax
from jax.experimental import pallas as pl
from jax.experimental.pallas import tpu as pltpu
from jax.sharding import PartitionSpec as P

SWEEPS = 2


def whitening(filter_taps):
    count = filter_taps.shape[0]
    padded = jnp.concatenate([filter_taps, jnp.zeros_like(filter_taps)])
    repeated = jnp.tile(padded, count)[: count * (2 * count - 1)]
    upper = repeated.reshape(count, 2 * count - 1)[:, :count]
    matrix = upper.T + jnp.eye(count, dtype=filter_taps.dtype)
    return matrix.astype(jnp.bfloat16)


def is_power_of_two(count):
    return count > 0 and count & (count - 1) == 0


def swap(block, axis, count, bit):
    return lax.ppermute(block, axis, [(i, i ^ bit) for i in range(count)])


def tree_sum(block, axis):
    count = lax.axis_size(axis)
    if not is_power_of_two(count):
        return lax.psum(block, axis)
    bit = 1
    while bit < count:
        block = block + swap(block, axis, count, bit)
        bit *= 2
    return block


def shift_sum(block, axis):
    count = lax.axis_size(axis)
    arrived = [
        lax.ppermute(block, axis, [(i, (i + shift) % count) for i in range(count)])
        for shift in range(1, count)
    ]
    for other in arrived:
        block = block + other
    return block


def tree_broadcast(block, fold_ratio, companion, on_first=None):
    row_count = lax.axis_size("row")
    col_count = lax.axis_size("col")
    owner = lax.axis_index("row") // fold_ratio
    offset = lax.axis_index("col") ^ owner
    if not is_power_of_two(col_count):
        block = jnp.where(offset == 0, block, jnp.zeros_like(block))
        return lax.psum(block, "col"), companion()
    bits = [1 << k for k in range(1, col_count.bit_length() - 1)] + [1][: col_count > 1]
    done = 0
    for bit in bits:
        pairs = []
        for row in range(row_count):
            base = row * col_count
            row_owner = row // fold_ratio
            for held in range(col_count):
                if (held ^ row_owner) & ~done == 0:
                    pairs.append((base + held, base + (held ^ bit)))
        arrived = lax.ppermute(block, ("row", "col"), pairs)
        done |= bit
        block = jnp.where((offset & ~done == 0) & (offset & bit != 0), arrived, block)
        block, companion = lax.optimization_barrier((block, companion()))
        companion = lambda held=companion: held
        if on_first is not None:
            block = on_first(block)
            on_first = None
    return block, companion()


def product_kernel(left_ref, right_ref, out_ref):
    out_ref[...] = lax.dot_general(
        left_ref[...], right_ref[...], (((0,), (0,)), ((), ())), preferred_element_type=jnp.float32
    )


def normal_rows(left, right, total_rows, first_row, previous):
    epochs, rows = left.shape
    width = right.shape[1]
    tile_rows = 128 if rows % 128 == 0 else rows
    tile_cols = width
    row_offset = first_row // tile_rows
    in_specs = [
        pl.BlockSpec((epochs, tile_rows), lambda j, i: (0, i)),
        pl.BlockSpec((epochs, tile_cols), lambda j, i: (0, j)),
    ]
    operands = [left, right]
    aliases = {}
    if previous is not None:
        in_specs.append(pl.BlockSpec(memory_space=pl.ANY))
        operands.append(previous)
        aliases = {2: 0}

    def kernel(left_ref, right_ref, *rest):
        product_kernel(left_ref, right_ref, rest[-1])

    return pl.pallas_call(
        kernel,
        grid=(width // tile_cols, rows // tile_rows),
        in_specs=in_specs,
        out_specs=pl.BlockSpec((tile_rows, tile_cols), lambda j, i: (i + row_offset, j)),
        out_shape=jax.ShapeDtypeStruct((total_rows, width), jnp.float32),
        input_output_aliases=aliases,
        compiler_params=pltpu.CompilerParams(vmem_limit_bytes=48 * 1024 * 1024),
        cost_estimate=pl.CostEstimate(
            flops=2 * rows * epochs * width,
            transcendentals=0,
            bytes_accessed=rows * width * 4 + epochs * width * 2 + rows * epochs * 2,
        ),
    )(*operands)


def contract_epochs(left, right):
    return lax.dot_general(
        left, right, (((0,), (0,)), ((), ())), precision=lax.Precision.HIGH
    )


def body(design, filter_taps, probes, lower_bound, upper_bound):
    row_count = lax.axis_size("row")
    col_count = lax.axis_size("col")
    fold_ratio = row_count // col_count
    row_index = lax.axis_index("row")
    panel_width = design.shape[1]
    row_width = panel_width // fold_ratio
    filter_matrix = whitening(filter_taps)
    whole_panel = lax.all_gather(design, "row", axis=0, tiled=True)
    white = jnp.dot(filter_matrix, whole_panel, preferred_element_type=jnp.float32).astype(
        jnp.bfloat16
    )
    first_column = row_index % fold_ratio * row_width
    half_rows = row_width // 2

    def whiten_rows(start):
        block = lax.dynamic_slice_in_dim(whole_panel, first_column + start, half_rows, 1)
        return jnp.dot(filter_matrix, block, preferred_element_type=jnp.float32).astype(jnp.bfloat16)


    def couple():
        white_wide = held["white"].astype(jnp.float32)
        panel_jacobi = jnp.sum(jnp.square(white_wide), axis=0) + 1e-06
        coupling = jnp.dot(
            white_wide / panel_jacobi[None, :], white_wide.T, precision=lax.Precision.HIGH
        )
        return tree_sum(coupling, "col")

    held = {}

    def release_second(block):
        held["second"], held["white"], block = lax.optimization_barrier(
            (whiten_rows(half_rows), white, block)
        )
        return block

    panel_first, _ = tree_broadcast(
        whiten_rows(0), fold_ratio, lambda: (), release_second
    )
    coupling = couple()
    panel_second, normal_tile = tree_broadcast(
        held["second"],
        fold_ratio,
        lambda: normal_rows(panel_first, white, row_width, 0, None),
    )
    normal_tile = normal_rows(panel_second, white, row_width, half_rows, normal_tile)
    panel = jnp.concatenate([panel_first, panel_second], axis=1)
    panel_wide = panel.astype(jnp.float32)
    jacobi = (jnp.sum(jnp.square(panel_wide), axis=0) + 1e-06)[:, None]
    center_value = (lower_bound[0] + upper_bound[0]) / 2.0
    half_width = (upper_bound[0] - lower_bound[0]) / 2.0
    sigma_value = center_value / half_width
    weight_now = 1.0 / sigma_value
    residual = probes
    scaled = residual / jacobi
    direction = scaled / center_value
    scaled_image = tree_sum(jnp.dot(panel_wide, scaled, precision=lax.Precision.HIGH), "row")
    image = scaled_image / center_value
    solution = jnp.zeros_like(residual)
    for sweep_index in range(SWEEPS):
        solution = solution + direction
        residual = residual - contract_epochs(panel_wide, image)
        weight_next = 1.0 / (2.0 * sigma_value - weight_now)
        direction = weight_next * weight_now * direction + 2.0 * weight_next / half_width * (
            residual / jacobi
        )
        if sweep_index + 1 < SWEEPS:
            scaled_image = scaled_image - jnp.dot(
                coupling, image, precision=lax.Precision.HIGH
            )
            image = weight_next * weight_now * image + 2.0 * weight_next / half_width * scaled_image
        weight_now = weight_next
    solution = solution + direction
    return (normal_tile, solution)


def solution(mesh):
    placed = (P("row", "col"), P(), P("row", "col"), P(), P())
    return jax.shard_map(
        body,
        mesh=mesh,
        in_specs=placed,
        out_specs=(P("row", "col"), P("row", "col")),
        check_vma=False,
    )
```

```python
import jax
import jax.numpy as jnp
from jax import lax
from jax.experimental import pallas as pl
from jax.experimental.pallas import tpu as pltpu
from jax.sharding import PartitionSpec as P

SWEEPS = 2


def whitening(filter_taps):
    count = filter_taps.shape[0]
    padded = jnp.concatenate([filter_taps, jnp.zeros_like(filter_taps)])
    repeated = jnp.tile(padded, count)[: count * (2 * count - 1)]
    upper = repeated.reshape(count, 2 * count - 1)[:, :count]
    matrix = upper.T + jnp.eye(count, dtype=filter_taps.dtype)
    return matrix.astype(jnp.bfloat16)


def is_power_of_two(count):
    return count > 0 and count & (count - 1) == 0


def swap(block, axis, count, bit):
    return lax.ppermute(block, axis, [(i, i ^ bit) for i in range(count)])


def tree_sum(block, axis):
    count = lax.axis_size(axis)
    if not is_power_of_two(count):
        return lax.psum(block, axis)
    bit = 1
    while bit < count:
        block = block + swap(block, axis, count, bit)
        bit *= 2
    return block


def shift_sum(block, axis):
    count = lax.axis_size(axis)
    arrived = [
        lax.ppermute(block, axis, [(i, (i + shift) % count) for i in range(count)])
        for shift in range(1, count)
    ]
    for other in arrived:
        block = block + other
    return block


def tree_broadcast(block, fold_ratio, companion, on_first=None):
    row_count = lax.axis_size("row")
    col_count = lax.axis_size("col")
    owner = lax.axis_index("row") // fold_ratio
    offset = lax.axis_index("col") ^ owner
    if not is_power_of_two(col_count):
        block = jnp.where(offset == 0, block, jnp.zeros_like(block))
        return lax.psum(block, "col"), companion()
    bits = [1 << k for k in range(1, col_count.bit_length() - 1)] + [1][: col_count > 1]
    done = 0
    for bit in bits:
        pairs = []
        for row in range(row_count):
            base = row * col_count
            row_owner = row // fold_ratio
            for held in range(col_count):
                if (held ^ row_owner) & ~done == 0:
                    pairs.append((base + held, base + (held ^ bit)))
        arrived = lax.ppermute(block, ("row", "col"), pairs)
        done |= bit
        block = jnp.where((offset & ~done == 0) & (offset & bit != 0), arrived, block)
        block, companion = lax.optimization_barrier((block, companion()))
        companion = lambda held=companion: held
        if on_first is not None:
            block = on_first(block)
            on_first = None
    return block, companion()


def product_kernel(left_ref, right_ref, out_ref):
    out_ref[...] = lax.dot_general(
        left_ref[...], right_ref[...], (((0,), (0,)), ((), ())), preferred_element_type=jnp.float32
    )


def normal_rows(left, right, total_rows, first_row, previous):
    epochs, rows = left.shape
    width = right.shape[1]
    tile_rows = 256 if rows % 256 == 0 else rows
    tile_cols = width // 2 if width % 256 == 0 else width
    row_offset = first_row // tile_rows
    in_specs = [
        pl.BlockSpec((epochs, tile_rows), lambda j, i: (0, i)),
        pl.BlockSpec((epochs, tile_cols), lambda j, i: (0, j)),
    ]
    operands = [left, right]
    aliases = {}
    if previous is not None:
        in_specs.append(pl.BlockSpec(memory_space=pl.ANY))
        operands.append(previous)
        aliases = {2: 0}

    def kernel(left_ref, right_ref, *rest):
        product_kernel(left_ref, right_ref, rest[-1])

    return pl.pallas_call(
        kernel,
        grid=(width // tile_cols, rows // tile_rows),
        in_specs=in_specs,
        out_specs=pl.BlockSpec((tile_rows, tile_cols), lambda j, i: (i + row_offset, j)),
        out_shape=jax.ShapeDtypeStruct((total_rows, width), jnp.float32),
        input_output_aliases=aliases,
        compiler_params=pltpu.CompilerParams(vmem_limit_bytes=48 * 1024 * 1024),
        cost_estimate=pl.CostEstimate(
            flops=2 * rows * epochs * width,
            transcendentals=0,
            bytes_accessed=rows * width * 4 + epochs * width * 2 + rows * epochs * 2,
        ),
    )(*operands)


def contract_epochs(left, right):
    return lax.dot_general(
        left, right, (((0,), (0,)), ((), ())), precision=lax.Precision.HIGH
    )


def body(design, filter_taps, probes, lower_bound, upper_bound):
    row_count = lax.axis_size("row")
    col_count = lax.axis_size("col")
    fold_ratio = row_count // col_count
    row_index = lax.axis_index("row")
    panel_width = design.shape[1]
    row_width = panel_width // fold_ratio
    filter_matrix = whitening(filter_taps)
    whole_panel = lax.all_gather(design, "row", axis=0, tiled=True)
    white = jnp.dot(filter_matrix, whole_panel, preferred_element_type=jnp.float32).astype(
        jnp.bfloat16
    )
    first_column = row_index % fold_ratio * row_width
    half_rows = row_width // 2

    def whiten_rows(start):
        block = lax.dynamic_slice_in_dim(whole_panel, first_column + start, half_rows, 1)
        return jnp.dot(filter_matrix, block, preferred_element_type=jnp.float32).astype(jnp.bfloat16)


    def couple():
        white_wide = held["white"].astype(jnp.float32)
        panel_jacobi = jnp.sum(jnp.square(white_wide), axis=0) + 1e-06
        coupling = jnp.dot(
            white_wide / panel_jacobi[None, :], white_wide.T, precision=lax.Precision.HIGH
        )
        return tree_sum(coupling, "col")

    held = {}

    def release_second(block):
        held["second"], held["white"], block = lax.optimization_barrier(
            (whiten_rows(half_rows), white, block)
        )
        return block

    panel_first, _ = tree_broadcast(
        whiten_rows(0), fold_ratio, lambda: (), release_second
    )
    coupling = couple()
    panel_second, normal_tile = tree_broadcast(
        held["second"],
        fold_ratio,
        lambda: normal_rows(panel_first, white, row_width, 0, None),
    )
    normal_tile = normal_rows(panel_second, white, row_width, half_rows, normal_tile)
    panel = jnp.concatenate([panel_first, panel_second], axis=1)
    panel_wide = panel.astype(jnp.float32)
    jacobi = (jnp.sum(jnp.square(panel_wide), axis=0) + 1e-06)[:, None]
    center_value = (lower_bound[0] + upper_bound[0]) / 2.0
    half_width = (upper_bound[0] - lower_bound[0]) / 2.0
    sigma_value = center_value / half_width
    weight_now = 1.0 / sigma_value
    residual = probes
    scaled = residual / jacobi
    direction = scaled / center_value
    scaled_image = tree_sum(jnp.dot(panel_wide, scaled, precision=lax.Precision.HIGH), "row")
    image = scaled_image / center_value
    solution = jnp.zeros_like(residual)
    for sweep_index in range(SWEEPS):
        solution = solution + direction
        residual = residual - contract_epochs(panel_wide, image)
        weight_next = 1.0 / (2.0 * sigma_value - weight_now)
        direction = weight_next * weight_now * direction + 2.0 * weight_next / half_width * (
            residual / jacobi
        )
        if sweep_index + 1 < SWEEPS:
            scaled_image = scaled_image - jnp.dot(
                coupling, image, precision=lax.Precision.HIGH
            )
            image = weight_next * weight_now * image + 2.0 * weight_next / half_width * scaled_image
        weight_now = weight_next
    solution = solution + direction
    return (normal_tile, solution)


def solution(mesh):
    placed = (P("row", "col"), P(), P("row", "col"), P(), P())
    return jax.shard_map(
        body,
        mesh=mesh,
        in_specs=placed,
        out_specs=(P("row", "col"), P("row", "col")),
        check_vma=False,
    )
```

```python
import jax
import jax.numpy as jnp
from jax import lax
from jax.experimental import pallas as pl
from jax.experimental.pallas import tpu as pltpu
from jax.sharding import PartitionSpec as P

SWEEPS = 2


def whitening(filter_taps):
    count = filter_taps.shape[0]
    padded = jnp.concatenate([filter_taps, jnp.zeros_like(filter_taps)])
    repeated = jnp.tile(padded, count)[: count * (2 * count - 1)]
    upper = repeated.reshape(count, 2 * count - 1)[:, :count]
    matrix = upper.T + jnp.eye(count, dtype=filter_taps.dtype)
    return matrix.astype(jnp.bfloat16)


def is_power_of_two(count):
    return count > 0 and count & (count - 1) == 0


def swap(block, axis, count, bit):
    return lax.ppermute(block, axis, [(i, i ^ bit) for i in range(count)])


def tree_sum(block, axis):
    count = lax.axis_size(axis)
    if not is_power_of_two(count):
        return lax.psum(block, axis)
    bit = 1
    while bit < count:
        block = block + swap(block, axis, count, bit)
        bit *= 2
    return block


def shift_sum(block, axis):
    count = lax.axis_size(axis)
    arrived = [
        lax.ppermute(block, axis, [(i, (i + shift) % count) for i in range(count)])
        for shift in range(1, count)
    ]
    for other in arrived:
        block = block + other
    return block


def tree_broadcast(block, fold_ratio, companion, on_first=None):
    row_count = lax.axis_size("row")
    col_count = lax.axis_size("col")
    owner = lax.axis_index("row") // fold_ratio
    offset = lax.axis_index("col") ^ owner
    if not is_power_of_two(col_count):
        block = jnp.where(offset == 0, block, jnp.zeros_like(block))
        return lax.psum(block, "col"), companion()
    bits = [1 << k for k in range(1, col_count.bit_length() - 1)] + [1][: col_count > 1]
    done = 0
    for bit in bits:
        pairs = []
        for row in range(row_count):
            base = row * col_count
            row_owner = row // fold_ratio
            for held in range(col_count):
                if (held ^ row_owner) & ~done == 0:
                    pairs.append((base + held, base + (held ^ bit)))
        arrived = lax.ppermute(block, ("row", "col"), pairs)
        done |= bit
        block = jnp.where((offset & ~done == 0) & (offset & bit != 0), arrived, block)
        block, companion = lax.optimization_barrier((block, companion()))
        companion = lambda held=companion: held
        if on_first is not None:
            block = on_first(block)
            on_first = None
    return block, companion()


def product_kernel(left_ref, right_ref, out_ref):
    out_ref[...] = lax.dot_general(
        left_ref[...], right_ref[...], (((0,), (0,)), ((), ())), preferred_element_type=jnp.float32
    )


def normal_rows(left, right, total_rows, first_row, previous):
    epochs, rows = left.shape
    width = right.shape[1]
    tile_rows = 384 if rows % 384 == 0 else rows
    tile_cols = width
    row_offset = first_row // tile_rows
    in_specs = [
        pl.BlockSpec((epochs, tile_rows), lambda j, i: (0, i)),
        pl.BlockSpec((epochs, tile_cols), lambda j, i: (0, j)),
    ]
    operands = [left, right]
    aliases = {}
    if previous is not None:
        in_specs.append(pl.BlockSpec(memory_space=pl.ANY))
        operands.append(previous)
        aliases = {2: 0}

    def kernel(left_ref, right_ref, *rest):
        product_kernel(left_ref, right_ref, rest[-1])

    return pl.pallas_call(
        kernel,
        grid=(width // tile_cols, rows // tile_rows),
        in_specs=in_specs,
        out_specs=pl.BlockSpec((tile_rows, tile_cols), lambda j, i: (i + row_offset, j)),
        out_shape=jax.ShapeDtypeStruct((total_rows, width), jnp.float32),
        input_output_aliases=aliases,
        compiler_params=pltpu.CompilerParams(vmem_limit_bytes=48 * 1024 * 1024),
        cost_estimate=pl.CostEstimate(
            flops=2 * rows * epochs * width,
            transcendentals=0,
            bytes_accessed=rows * width * 4 + epochs * width * 2 + rows * epochs * 2,
        ),
    )(*operands)


def contract_epochs(left, right):
    return lax.dot_general(
        left, right, (((0,), (0,)), ((), ())), precision=lax.Precision.HIGH
    )


def body(design, filter_taps, probes, lower_bound, upper_bound):
    row_count = lax.axis_size("row")
    col_count = lax.axis_size("col")
    fold_ratio = row_count // col_count
    row_index = lax.axis_index("row")
    panel_width = design.shape[1]
    row_width = panel_width // fold_ratio
    filter_matrix = whitening(filter_taps)
    whole_panel = lax.all_gather(design, "row", axis=0, tiled=True)
    white = jnp.dot(filter_matrix, whole_panel, preferred_element_type=jnp.float32).astype(
        jnp.bfloat16
    )
    first_column = row_index % fold_ratio * row_width
    half_rows = row_width // 2

    def whiten_rows(start):
        block = lax.dynamic_slice_in_dim(whole_panel, first_column + start, half_rows, 1)
        return jnp.dot(filter_matrix, block, preferred_element_type=jnp.float32).astype(jnp.bfloat16)


    def couple():
        white_wide = held["white"].astype(jnp.float32)
        panel_jacobi = jnp.sum(jnp.square(white_wide), axis=0) + 1e-06
        coupling = jnp.dot(
            white_wide / panel_jacobi[None, :], white_wide.T, precision=lax.Precision.HIGH
        )
        return tree_sum(coupling, "col")

    held = {}

    def release_second(block):
        held["second"], held["white"], block = lax.optimization_barrier(
            (whiten_rows(half_rows), white, block)
        )
        return block

    panel_first, _ = tree_broadcast(
        whiten_rows(0), fold_ratio, lambda: (), release_second
    )
    coupling = couple()
    panel_second, normal_tile = tree_broadcast(
        held["second"],
        fold_ratio,
        lambda: normal_rows(panel_first, white, row_width, 0, None),
    )
    normal_tile = normal_rows(panel_second, white, row_width, half_rows, normal_tile)
    panel = jnp.concatenate([panel_first, panel_second], axis=1)
    panel_wide = panel.astype(jnp.float32)
    jacobi = (jnp.sum(jnp.square(panel_wide), axis=0) + 1e-06)[:, None]
    center_value = (lower_bound[0] + upper_bound[0]) / 2.0
    half_width = (upper_bound[0] - lower_bound[0]) / 2.0
    sigma_value = center_value / half_width
    weight_now = 1.0 / sigma_value
    residual = probes
    scaled = residual / jacobi
    direction = scaled / center_value
    scaled_image = tree_sum(jnp.dot(panel_wide, scaled, precision=lax.Precision.HIGH), "row")
    image = scaled_image / center_value
    solution = jnp.zeros_like(residual)
    for sweep_index in range(SWEEPS):
        solution = solution + direction
        residual = residual - contract_epochs(panel_wide, image)
        weight_next = 1.0 / (2.0 * sigma_value - weight_now)
        direction = weight_next * weight_now * direction + 2.0 * weight_next / half_width * (
            residual / jacobi
        )
        if sweep_index + 1 < SWEEPS:
            scaled_image = scaled_image - jnp.dot(
                coupling, image, precision=lax.Precision.HIGH
            )
            image = weight_next * weight_now * image + 2.0 * weight_next / half_width * scaled_image
        weight_now = weight_next
    solution = solution + direction
    return (normal_tile, solution)


def solution(mesh):
    placed = (P("row", "col"), P(), P("row", "col"), P(), P())
    return jax.shard_map(
        body,
        mesh=mesh,
        in_specs=placed,
        out_specs=(P("row", "col"), P("row", "col")),
        check_vma=False,
    )
```
